768 devices in a mesh: chan: 12 (over z), tile: 64 (over x, y, core).
Axes of the slice: x: 4, y: 8, z: 12, core: 2. Of those that a mesh axis runs over, the one named last changes fastest.
Arguments:
- samples: float32 [64, 48, 12, 2, 128], P('tile', 'chan'), may hold values from -6 to 6
- uv_coords: float32 [64, 48, 12, 2, 128], P('tile', 'chan'), may hold values from 4 to 28
- block_owner: int32 [64, 48, 1], P('tile', 'chan'), may hold values from 0 to 63; in each aligned block of 48 rows (0 to 47, 48 to 95, ..., all dimensions but the last counted through in order) at most 2 rows name the same one
- placement_map: int32 [64, 48, 2], P('tile', 'chan'), may hold values from 0 to 2016, as said below
- block_count: int32 [64, 12], P('tile', 'chan'), may hold values from 2 to 4, as said below
Outputs:
- dirty_image: float32 [12, 2048, 2048], P('chan', 'tile')
The draws below stay inside these ranges and needn't reach their ends.
Inputs may be any that keep to these rules, and one draw needn't show every extreme that they name: `block_owner`: in each row of 48 blocks (one tile index), no owner is named by more than 2 blocks, a bound that some block reaches. `placement_map`: component 0 is at most 0, component 1 at most 2016; that column is reached in every draw. `block_count`: some device holds 4 blocks with data in every draw.
All inputs are finite; a program needn't handle non-finite values.
Results may differ from the reference program's by a relative error of at most 0.0029.
Values may be sent and summed in bfloat16 or wider, within the bound.
No kernel may reach another device: no remote copies, remote signals or barrier semaphores. Data moves between devices by JAX's collectives and lax.ppermute only.
A program may use at most 32 MiB of HBM per device.

```python
import math
from functools import partial
import jax
import jax.numpy as jnp
import numpy as np
from jax import lax

G = 2048
NS = 32
TS = 128
NB = 4
CH = 12
BLK_GROUP = 48
BAND = 32
CAP = 2
N_CHAN = 12
N_TILE = 64


def draw_placement_map(key, part):
    key_rows = jax.random.fold_in(key, 11)
    key_cols = jax.random.fold_in(key, 12)
    key_pick = jax.random.fold_in(key, 13)
    row_start = jax.random.randint(key_rows, (N_TILE, BLK_GROUP), 0, BAND - NS + 1)
    col_start = jax.random.randint(key_cols, (N_TILE, BLK_GROUP), 0, G - NS + 1)
    chosen = jax.random.randint(key_pick, (), 0, N_TILE * BLK_GROUP)
    flat_index = jnp.arange(N_TILE * BLK_GROUP).reshape(N_TILE, BLK_GROUP)
    col_start = jnp.where(flat_index == chosen, G - NS, col_start)
    return jnp.stack([row_start, col_start], axis=-1).astype(jnp.int32)


def draw_block_count(key, part):
    key_count = jax.random.fold_in(key, 21)
    key_pick = jax.random.fold_in(key, 22)
    counts = jax.random.randint(key_count, (N_TILE * N_CHAN,), max(1, NB // 2), NB + 1)
    chosen = jax.random.randint(key_pick, (), 0, N_TILE * N_CHAN)
    counts = jnp.where(jnp.arange(N_TILE * N_CHAN) == chosen, NB, counts)
    return counts.reshape(N_TILE, N_CHAN).astype(jnp.int32)


def block_scale(key, shape, cuts, least, high):
    level = 1.0
    for dim, blocks in cuts:
        draws = jax.random.uniform(jax.random.fold_in(jax.random.fold_in(key, 6), dim), (blocks,), jnp.float32, least / len(cuts), high / len(cuts))
        level = level * jnp.repeat(jnp.exp(draws), shape[dim] // blocks).reshape((-1,) + (1,) * (len(shape) - 1 - dim))
    return level


def assign_block(rng, own, number, rows, amount, top, most, skew):
    sequence = jax.random.permutation(rng, amount)
    packed, usual = load_shares(amount, rows * top, most, skew, True), load_shares(amount, rows * top, most, skew, False)
    places = jnp.arange(amount)

    def named(sizes, rotation):
        used = int((sizes > 0).sum())
        fixed = max(1, used // 4)
        shifted = fixed + (places - fixed + rotation * (used - fixed)) % max(1, amount - fixed)
        return jnp.zeros((amount,), jnp.int32).at[sequence[jnp.where(places < fixed, places, shifted)]].set(jnp.asarray(sizes, jnp.int32))

    sizes = jnp.where(number % 4 == 0, named(packed, number // 4), named(usual, number - number // 4 - 1))
    mixed = jax.random.permutation(jax.random.fold_in(own, 3), amount)
    donor, taker = mixed[0:amount // 2 * 2:2], mixed[1:amount // 2 * 2:2]
    margin = jnp.minimum(sizes[donor] - 1, most - sizes[taker]) // 2
    margin = jnp.where((donor == sequence[0]) | (taker == sequence[0]) | (sizes[taker] == 0), 0, jnp.maximum(margin, 0))
    shifted = jax.random.randint(jax.random.fold_in(own, 4), (amount // 2,), 0, 1 << 20) % (margin + 1)
    sizes = sizes.at[donor].add(-shifted).at[taker].add(shifted)
    members = jnp.searchsorted(jnp.cumsum(sizes), jnp.arange(rows * top), side="right").astype(jnp.int32)
    listing = members.reshape(top, rows).T
    listing = listing[jax.random.permutation(jax.random.fold_in(own, 1), rows)]
    rotation = jax.random.randint(jax.random.fold_in(own, 2), (rows, 1), 0, top)
    return jnp.take_along_axis(listing, (jnp.arange(top)[None, :] + rotation) % top, axis=1)


def load_shares(amount, total, bound, lean, full):
    weights = [(1 << 20) // math.isqrt(standing ** lean) + 1 for standing in range(1, amount + 1)]
    largest = bound if full else min(bound, max(-(-total // amount), total * weights[0] // sum(weights)))
    least = 1 if total - largest >= amount - 1 else 0
    given, surplus = [largest] + [least] * (amount - 1), total - largest - least * (amount - 1)
    while surplus > 0:
        candidates = [i for i in range(1, amount) if given[i] < largest] or [i for i in range(1, amount) if given[i] < bound]
        mass, remaining = sum([weights[i] for i in candidates]), surplus
        for i in candidates:
            addition = min(bound - given[i], max(1, remaining * weights[i] // mass), surplus)
            given[i] = given[i] + addition
            surplus = surplus - addition
    return np.array(given)


def normal_values(rng, dims, spread, most, split=(), dtype=jnp.bfloat16):
    drawn = jax.random.normal(rng, dims, jnp.float32) * spread
    if len(split) > 0:
        drawn = block_scale(rng, dims, split, -0.22, 0.18) * drawn
    return jnp.clip(drawn, min=-most, max=most).astype(dtype)


def setup_inputs(seed: int = 0) -> dict:
    arg_keys = jax.random.split(jax.random.key(seed), 6)
    samples = normal_values(arg_keys[0], (N_TILE, BLK_GROUP, CH, 2, TS), 1.0, 6.0, ((0, 64), (1, 12)), jnp.float32)
    uv_coords = jnp.clip(4.0 + 24.0 * jax.random.uniform(arg_keys[1], (N_TILE, BLK_GROUP, CH, 2, TS), jnp.float32) ** block_scale(arg_keys[1], (N_TILE, BLK_GROUP, CH, 2, TS), ((0, 64), (1, 12)), -0.2, 0.2), 4.0, 28.0)
    block_owner_keys = jax.random.split(jax.random.fold_in(arg_keys[2], 1), N_TILE * BLK_GROUP // BLK_GROUP)
    block_owner_turns = jax.random.permutation(jax.random.fold_in(arg_keys[2], 3), N_TILE * BLK_GROUP // BLK_GROUP)
    block_owner = jax.vmap(lambda own, number: assign_block(jax.random.fold_in(arg_keys[2], 2), own, number, BLK_GROUP, N_TILE, 1, CAP, 2))(block_owner_keys, block_owner_turns).reshape((N_TILE, BLK_GROUP, 1))
    placement_map = draw_placement_map(jax.random.fold_in(arg_keys[5], 71), 0)
    block_count = draw_block_count(jax.random.fold_in(arg_keys[5], 71), 0)
    return {"samples": samples, "uv_coords": uv_coords, "block_owner": block_owner, "placement_map": placement_map, "block_count": block_count}


def complex_einsum(pattern, left_real, left_imag, right_real, right_imag):
    product = partial(jnp.einsum, pattern, precision=lax.Precision.HIGHEST)
    real_part = product(left_real, right_real) - product(left_imag, right_imag)
    imag_part = product(left_real, right_imag) + product(left_imag, right_real)
    return real_part, imag_part


def phase_table(row_count, col_count, length, sign):
    index = (jnp.arange(row_count)[:, None] * jnp.arange(col_count)[None, :]) % length
    angle = (sign * 2.0 * math.pi / length) * index.astype(jnp.float32)
    return jnp.cos(angle), jnp.sin(angle)


def form_subgrids(masked, coords):
    offset = jnp.arange(NS).astype(jnp.float32) - NS / 2.0
    factor = 2.0 * math.pi / NS
    angle_u = coords[:, 0, :, None] * offset[None, None, :] * factor
    angle_v = coords[:, 1, :, None] * offset[None, None, :] * factor
    cos_u = jnp.cos(angle_u)
    sin_u = jnp.sin(angle_u)
    vis_real = masked[:, 0, :, None]
    vis_imag = masked[:, 1, :, None]
    weight_real = vis_real * cos_u - vis_imag * sin_u
    weight_imag = vis_real * sin_u + vis_imag * cos_u
    image_real, image_imag = complex_einsum("ikx,iky->ixy", weight_real, weight_imag, jnp.cos(angle_v), jnp.sin(angle_v))
    table_real, table_imag = phase_table(NS, NS, NS, -1.0)
    half_real, half_imag = complex_einsum("ixy,yq->ixq", image_real, image_imag, table_real, table_imag)
    full_real, full_imag = complex_einsum("px,ixq->ipq", table_real, table_imag, half_real, half_imag)
    stacked = jnp.stack([full_real, full_imag], axis=1) / (NS * NS)
    return stacked.astype(jnp.bfloat16)


def reference(samples, uv_coords, block_owner, placement_map, block_count):
    position = jnp.arange(BLK_GROUP).astype(jnp.int32)
    limit = block_count[:, position // NB]
    live_mask = ((position % NB)[None, :] < limit).astype(jnp.float32)
    masked = samples * live_mask[:, :, None, None, None]
    first_rows = block_owner[:, :, 0] * BAND + placement_map[:, :, 0]
    first_cols = placement_map[:, :, 1]
    inner = jnp.arange(NS).astype(jnp.int32)

    def add_group(uv_grid, group_items):
        group_samples, group_coords, row_start, col_start = group_items
        formed = form_subgrids(group_samples.reshape(BLK_GROUP * CH, 2, TS), group_coords.reshape(BLK_GROUP * CH, 2, TS))
        formed = lax.optimization_barrier(formed)
        formed = formed.astype(jnp.float32).reshape(BLK_GROUP, CH, 2, NS, NS)
        row_index = jnp.broadcast_to(row_start[:, None, None] + inner[None, :, None], (BLK_GROUP, NS, NS))
        col_index = jnp.broadcast_to(col_start[:, None, None] + inner[None, None, :], (BLK_GROUP, NS, NS))
        values = jnp.transpose(formed, (1, 2, 0, 3, 4))
        return uv_grid.at[:, :, row_index, col_index].add(values), None

    start = jnp.zeros((CH, 2, G, G), jnp.float32)
    uv_grid, unused = lax.scan(add_group, start, (masked, uv_coords, first_rows, first_cols))
    complex_grid = uv_grid[:, 0] + 1j * uv_grid[:, 1]
    flipped = jnp.real(jnp.fft.ifft2(complex_grid, axes=(1, 2))) * G
    return jnp.swapaxes(flipped, 1, 2).astype(jnp.float32)
```

```python
import math

import jax
import jax.numpy as jnp
from jax import lax
from jax.sharding import PartitionSpec as P

G = 2048
NS = 32
META = 128
HIGH = lax.Precision.HIGH
HIGHEST = lax.Precision.HIGHEST


def phase_table(row_count, col_count, length, sign):
    index = jnp.arange(row_count)[:, None] * jnp.arange(col_count)[None, :] % length
    angle = sign * 2.0 * math.pi / length * index.astype(jnp.float32)
    return (jnp.cos(angle), jnp.sin(angle))


def block_matrix(real, imag):
    return jnp.stack([jnp.stack([real, -imag]), jnp.stack([imag, real])])


def offset_phase(coord):
    factor = 2.0 * math.pi / NS
    coarse = (8.0 * jnp.arange(4) - NS / 2.0).astype(jnp.float32)
    fine = jnp.arange(8).astype(jnp.float32)
    angle_c = coord[..., None] * coarse * factor
    angle_f = coord[..., None] * fine * factor
    cos_c, sin_c = jnp.cos(angle_c)[..., :, None], jnp.sin(angle_c)[..., :, None]
    cos_f, sin_f = jnp.cos(angle_f)[..., None, :], jnp.sin(angle_f)[..., None, :]
    real = cos_c * cos_f - sin_c * sin_f
    imag = sin_c * cos_f + cos_c * sin_f
    shape = coord.shape + (NS,)
    return real.reshape(shape), imag.reshape(shape)


def form_subgrids(masked, coords):
    count = masked.shape[0]
    cos_u, sin_u = offset_phase(coords[:, 0])
    cos_v, sin_v = offset_phase(coords[:, 1])
    vis_real = masked[:, 0, :, None]
    vis_imag = masked[:, 1, :, None]
    weight_real = vis_real * cos_u - vis_imag * sin_u
    weight_imag = vis_real * sin_u + vis_imag * cos_u
    left = jnp.concatenate([weight_real, weight_imag], axis=1)
    right = jnp.concatenate(
        [jnp.concatenate([cos_v, sin_v], axis=2), jnp.concatenate([-sin_v, cos_v], axis=2)], axis=1
    )
    image = jnp.einsum("ikx,iky->ixy", left, right, precision=HIGH)
    image = image.reshape(count, NS, 2, NS)
    table = block_matrix(*phase_table(NS, NS, NS, -1.0))
    half = jnp.einsum("ixcy,ocyq->ixoq", image, table, precision=HIGHEST)
    full = jnp.einsum("ocpx,ixcq->iopq", table, half, precision=HIGHEST)
    return (full / (NS * NS)).astype(jnp.bfloat16)


def slot_targets(owners, tile_count, capacity):
    onehot = (owners[:, None] == jnp.arange(tile_count)[None, :]).astype(jnp.int32)
    before = jnp.cumsum(onehot, axis=0) - onehot
    slot_rank = jnp.sum(before * onehot, axis=1)
    return owners * capacity + slot_rank


def place_windows(windows, col_hi, col_lo, col_blocks):
    slots = windows.shape[0]
    wide = jnp.arange(2 * NS)
    shift = (wide[None, None, :] == col_lo[:, None, None] + jnp.arange(NS)[None, :, None])
    shifted = jnp.einsum(
        "scpq,sqw->scpw", windows, shift.astype(jnp.bfloat16), preferred_element_type=jnp.float32
    ).astype(jnp.bfloat16)
    shifted = shifted.reshape(slots, 2, NS, 2, NS)
    hit = jnp.arange(col_blocks)[:, None, None] == col_hi[None, :, None] + jnp.arange(2)[None, None, :]
    grid = jnp.einsum(
        "bsk,scpka->cpba", hit.astype(jnp.bfloat16), shifted, preferred_element_type=jnp.float32
    )
    return grid.reshape(2, NS, col_blocks * NS)


def factor_lengths(length):
    outer_len = 2 ** ((length.bit_length() - 1) // 2)
    return (outer_len, length // outer_len)


def transform_rows(grid):
    rows = grid.shape[1]
    outer_len, inner_len = factor_lengths(G)
    split = grid.reshape(2, rows, inner_len, outer_len)
    first = block_matrix(*phase_table(inner_len, inner_len, inner_len, 1.0))
    section = jnp.einsum("opba,Pobc->Pcpa", split, first, precision=HIGH)
    twiddle_real, twiddle_imag = phase_table(inner_len, outer_len, G, 1.0)
    twiddle_real = twiddle_real[:, None, :]
    twiddle_imag = twiddle_imag[:, None, :]
    turned_real = section[0] * twiddle_real - section[1] * twiddle_imag
    turned_imag = section[0] * twiddle_imag + section[1] * twiddle_real
    turned = jnp.stack([turned_real, turned_imag])
    second = block_matrix(*phase_table(outer_len, outer_len, outer_len, 1.0))
    return jnp.einsum("Ocpa,POad->dcPp", turned, second, precision=HIGH)


def transform_cols(turned):
    outer_len, inner_len = factor_lengths(G)
    first = block_matrix(*phase_table(inner_len, inner_len, inner_len, 1.0))
    section = jnp.einsum("bmoa,Pobc->Pcma", turned, first, precision=HIGH)
    twiddle_real, twiddle_imag = phase_table(inner_len, outer_len, G, 1.0)
    twiddle_real = twiddle_real[:, None, :]
    twiddle_imag = twiddle_imag[:, None, :]
    turned_real = section[0] * twiddle_real - section[1] * twiddle_imag
    turned_imag = section[0] * twiddle_imag + section[1] * twiddle_real
    second_real, second_imag = phase_table(outer_len, outer_len, outer_len, 1.0)
    second = jnp.stack([second_real, -second_imag])
    stacked = jnp.stack([turned_real, turned_imag])
    final = jnp.einsum("ocma,oad->mdc", stacked, second, precision=HIGH)
    return final.reshape(final.shape[0], G)


def per_device(samples, uv_coords, block_owner, placement_map, block_count):
    chan_count = lax.axis_size("chan")
    tile_count = lax.axis_size("tile")
    blocks = samples.shape[1]
    channels = samples.shape[2]
    steps_time = samples.shape[-1]
    group_blocks = blocks * chan_count
    capacity = max(2, 2 * group_blocks // tile_count)
    band_rows = G // tile_count
    live_mask = (jnp.arange(blocks) < block_count.reshape(())).astype(jnp.float32)
    masked = samples[0] * live_mask[:, None, None, None]
    item_count = blocks * channels
    formed = form_subgrids(
        masked.reshape(item_count, 2, steps_time), uv_coords[0].reshape(item_count, 2, steps_time)
    )
    cell_count = 2 * NS * NS
    formed = formed.reshape(blocks, channels, cell_count)
    owners = block_owner[0, :, 0]
    cols = placement_map[0, :, 1]
    meta = jnp.stack([owners, cols // NS, cols % NS], axis=1).astype(jnp.bfloat16)
    meta = jnp.pad(meta, ((0, 0), (0, META - 3)))
    meta = jnp.broadcast_to(meta[:, None, :], (blocks, channels, META))
    payload = jnp.concatenate([formed, meta], axis=2)
    arrived = lax.all_to_all(payload, "chan", split_axis=1, concat_axis=0, tiled=True)
    arrived = arrived.reshape(group_blocks, cell_count + META)
    group_owners = arrived[:, cell_count].astype(jnp.int32)
    target = slot_targets(group_owners, tile_count, capacity)
    slot_count = tile_count * capacity
    pick = (jnp.arange(slot_count)[:, None] == target[None, :]).astype(jnp.bfloat16)
    outgoing = jnp.dot(pick, arrived, preferred_element_type=jnp.float32).astype(jnp.bfloat16)
    incoming = lax.all_to_all(outgoing, "tile", split_axis=0, concat_axis=0, tiled=True)
    windows = incoming[:, :cell_count].reshape(slot_count, 2, NS, NS)
    col_hi = incoming[:, cell_count + 1].astype(jnp.int32)
    col_lo = incoming[:, cell_count + 2].astype(jnp.int32)
    tile_grid = place_windows(windows, col_hi, col_lo, G // NS)
    half = transform_rows(tile_grid)
    half = half.reshape(tile_count, G // tile_count, 2, band_rows)
    turned = lax.all_to_all(half, "tile", split_axis=0, concat_axis=0, tiled=True)
    dirty_image = transform_cols(turned) / G
    return dirty_image[None]


def solution(mesh):
    in_specs = (
        P("tile", "chan", None, None, None),
        P("tile", "chan", None, None, None),
        P("tile", "chan", None),
        P("tile", "chan", None),
        P("tile", "chan"),
    )
    out_specs = P("chan", "tile", None)
    return jax.shard_map(
        per_device, mesh=mesh, in_specs=in_specs, out_specs=out_specs, check_vma=False
    )
```

```python
import math

import jax
import jax.numpy as jnp
from jax import lax
from jax.sharding import PartitionSpec as P

G = 2048
NS = 32
META = 128
HIGH = lax.Precision.HIGH
HIGHEST = lax.Precision.HIGHEST


def phase_table(row_count, col_count, length, sign):
    index = jnp.arange(row_count)[:, None] * jnp.arange(col_count)[None, :] % length
    angle = sign * 2.0 * math.pi / length * index.astype(jnp.float32)
    return (jnp.cos(angle), jnp.sin(angle))


def block_matrix(real, imag):
    return jnp.stack([jnp.stack([real, -imag]), jnp.stack([imag, real])])


def offset_phase(coord):
    factor = 2.0 * math.pi / NS
    coarse = (8.0 * jnp.arange(4) - NS / 2.0).astype(jnp.float32)
    fine = jnp.arange(8).astype(jnp.float32)
    angle_c = coord[..., None] * coarse * factor
    angle_f = coord[..., None] * fine * factor
    cos_c, sin_c = jnp.cos(angle_c)[..., :, None], jnp.sin(angle_c)[..., :, None]
    cos_f, sin_f = jnp.cos(angle_f)[..., None, :], jnp.sin(angle_f)[..., None, :]
    real = cos_c * cos_f - sin_c * sin_f
    imag = sin_c * cos_f + cos_c * sin_f
    shape = coord.shape + (NS,)
    return real.reshape(shape), imag.reshape(shape)


def form_subgrids(masked, coords):
    count = masked.shape[0]
    cos_u, sin_u = offset_phase(coords[:, 0])
    cos_v, sin_v = offset_phase(coords[:, 1])
    vis_real = masked[:, 0, :, None]
    vis_imag = masked[:, 1, :, None]
    weight_real = vis_real * cos_u - vis_imag * sin_u
    weight_imag = vis_real * sin_u + vis_imag * cos_u
    left = jnp.concatenate([weight_real, weight_imag], axis=1)
    right = jnp.concatenate(
        [jnp.concatenate([cos_v, sin_v], axis=2), jnp.concatenate([-sin_v, cos_v], axis=2)], axis=1
    )
    image = jnp.einsum("ikx,iky->ixy", left, right, precision=HIGH)
    image = image.reshape(count, NS, 2, NS)
    table = block_matrix(*phase_table(NS, NS, NS, -1.0))
    half = jnp.einsum("ixcy,ocyq->ixoq", image, table, precision=HIGHEST)
    full = jnp.einsum("ocpx,ixcq->iopq", table, half, precision=HIGHEST)
    return (full / (NS * NS)).astype(jnp.bfloat16)


def slot_targets(owners, tile_count, capacity):
    onehot = (owners[:, None] == jnp.arange(tile_count)[None, :]).astype(jnp.int32)
    before = jnp.cumsum(onehot, axis=0) - onehot
    slot_rank = jnp.sum(before * onehot, axis=1)
    return owners * capacity + slot_rank


def place_windows(windows, col_hi, col_lo, col_blocks):
    slots = windows.shape[0]
    wide = jnp.arange(2 * NS)
    shift = (wide[None, None, :] == col_lo[:, None, None] + jnp.arange(NS)[None, :, None])
    shifted = jnp.einsum(
        "scpq,sqw->scpw", windows, shift.astype(jnp.bfloat16), preferred_element_type=jnp.float32
    ).astype(jnp.bfloat16)
    shifted = shifted.reshape(slots, 2, NS, 2, NS)
    hit = jnp.arange(col_blocks)[:, None, None] == col_hi[None, :, None] + jnp.arange(2)[None, None, :]
    grid = jnp.einsum(
        "bsk,scpka->cpba", hit.astype(jnp.bfloat16), shifted, preferred_element_type=jnp.float32
    )
    return grid.reshape(2, NS, col_blocks * NS)


def factor_lengths(length):
    outer_len = 2 ** ((length.bit_length() - 1) // 2)
    return (outer_len, length // outer_len)


def transform_rows(grid):
    rows = grid.shape[1]
    outer_len, inner_len = factor_lengths(G)
    split = grid.reshape(2, rows, inner_len, outer_len)
    first = block_matrix(*phase_table(inner_len, inner_len, inner_len, 1.0))
    section = jnp.einsum("opba,Pobc->Pcpa", split, first, precision=HIGH)
    twiddle_real, twiddle_imag = phase_table(inner_len, outer_len, G, 1.0)
    twiddle_real = twiddle_real[:, None, :]
    twiddle_imag = twiddle_imag[:, None, :]
    turned_real = section[0] * twiddle_real - section[1] * twiddle_imag
    turned_imag = section[0] * twiddle_imag + section[1] * twiddle_real
    turned = jnp.stack([turned_real, turned_imag])
    second = block_matrix(*phase_table(outer_len, outer_len, outer_len, 1.0))
    return jnp.einsum("Ocpa,POad->dcPp", turned, second, precision=HIGH)


def transform_cols(turned):
    outer_len, inner_len = factor_lengths(G)
    first = block_matrix(*phase_table(inner_len, inner_len, inner_len, 1.0))
    section = jnp.einsum("bmoa,Pobc->Pcma", turned, first, precision=HIGH)
    twiddle_real, twiddle_imag = phase_table(inner_len, outer_len, G, 1.0)
    twiddle_real = twiddle_real[:, None, :]
    twiddle_imag = twiddle_imag[:, None, :]
    turned_real = section[0] * twiddle_real - section[1] * twiddle_imag
    turned_imag = section[0] * twiddle_imag + section[1] * twiddle_real
    second_real, second_imag = phase_table(outer_len, outer_len, outer_len, 1.0)
    second = jnp.stack([second_real, -second_imag])
    stacked = jnp.stack([turned_real, turned_imag])
    final = jnp.einsum("ocma,oad->mdc", stacked, second, precision=HIGH)
    return final.reshape(final.shape[0], G)


def per_device(samples, uv_coords, block_owner, placement_map, block_count):
    chan_count = lax.axis_size("chan")
    tile_count = lax.axis_size("tile")
    blocks = samples.shape[1]
    channels = samples.shape[2]
    steps_time = samples.shape[-1]
    group_blocks = blocks * chan_count
    capacity = max(2, 2 * group_blocks // tile_count)
    band_rows = G // tile_count
    live_mask = (jnp.arange(blocks) < block_count.reshape(())).astype(jnp.float32)
    masked = samples[0] * live_mask[:, None, None, None]
    owners = block_owner[0, :, 0]
    cols = placement_map[0, :, 1]
    meta = jnp.stack([owners, cols // NS, cols % NS], axis=1).astype(jnp.float32)
    meta = jnp.pad(meta, ((0, 0), (0, steps_time - 3)))
    meta = jnp.broadcast_to(meta[:, None, None, :], (blocks, channels, 1, steps_time))
    payload = jnp.concatenate([masked, uv_coords[0], meta], axis=2)
    arrived = lax.all_to_all(payload, "chan", split_axis=1, concat_axis=0, tiled=True)
    arrived = arrived.reshape(group_blocks, 5, steps_time)
    formed = form_subgrids(arrived[:, 0:2], arrived[:, 2:4])
    cell_count = 2 * NS * NS
    group_meta = arrived[:, 4, 0:META].astype(jnp.bfloat16)
    arrived = jnp.concatenate([formed.reshape(group_blocks, cell_count), group_meta], axis=1)
    group_owners = group_meta[:, 0].astype(jnp.int32)
    target = slot_targets(group_owners, tile_count, capacity)
    slot_count = tile_count * capacity
    pick = (jnp.arange(slot_count)[:, None] == target[None, :]).astype(jnp.bfloat16)
    outgoing = jnp.dot(pick, arrived, preferred_element_type=jnp.float32).astype(jnp.bfloat16)
    incoming = lax.all_to_all(outgoing, "tile", split_axis=0, concat_axis=0, tiled=True)
    windows = incoming[:, :cell_count].reshape(slot_count, 2, NS, NS)
    col_hi = incoming[:, cell_count + 1].astype(jnp.int32)
    col_lo = incoming[:, cell_count + 2].astype(jnp.int32)
    tile_grid = place_windows(windows, col_hi, col_lo, G // NS)
    half = transform_rows(tile_grid)
    half = half.reshape(tile_count, G // tile_count, 2, band_rows)
    turned = lax.all_to_all(half, "tile", split_axis=0, concat_axis=0, tiled=True)
    dirty_image = transform_cols(turned) / G
    return dirty_image[None]


def solution(mesh):
    in_specs = (
        P("tile", "chan", None, None, None),
        P("tile", "chan", None, None, None),
        P("tile", "chan", None),
        P("tile", "chan", None),
        P("tile", "chan"),
    )
    out_specs = P("chan", "tile", None)
    return jax.shard_map(
        per_device, mesh=mesh, in_specs=in_specs, out_specs=out_specs, check_vma=False
    )
```

```python
import math

import jax
import jax.numpy as jnp
from jax import lax
from jax.sharding import PartitionSpec as P

G = 2048
NS = 32
META = 128
HIGH = lax.Precision.HIGH
HIGHEST = lax.Precision.HIGHEST


def phase_table(row_count, col_count, length, sign):
    index = jnp.arange(row_count)[:, None] * jnp.arange(col_count)[None, :] % length
    angle = sign * 2.0 * math.pi / length * index.astype(jnp.float32)
    return (jnp.cos(angle), jnp.sin(angle))


def block_matrix(real, imag):
    return jnp.stack([jnp.stack([real, -imag]), jnp.stack([imag, real])])


def offset_phase(coord):
    factor = 2.0 * math.pi / NS
    coarse = (8.0 * jnp.arange(4) - NS / 2.0).astype(jnp.float32)
    fine = jnp.arange(8).astype(jnp.float32)
    angle_c = coord[..., None] * coarse * factor
    angle_f = coord[..., None] * fine * factor
    cos_c, sin_c = jnp.cos(angle_c)[..., :, None], jnp.sin(angle_c)[..., :, None]
    cos_f, sin_f = jnp.cos(angle_f)[..., None, :], jnp.sin(angle_f)[..., None, :]
    real = cos_c * cos_f - sin_c * sin_f
    imag = sin_c * cos_f + cos_c * sin_f
    shape = coord.shape + (NS,)
    return real.reshape(shape), imag.reshape(shape)


def form_subgrids(masked, coords):
    count = masked.shape[0]
    cos_u, sin_u = offset_phase(coords[:, 0])
    cos_v, sin_v = offset_phase(coords[:, 1])
    vis_real = masked[:, 0, :, None]
    vis_imag = masked[:, 1, :, None]
    weight_real = vis_real * cos_u - vis_imag * sin_u
    weight_imag = vis_real * sin_u + vis_imag * cos_u
    left = jnp.concatenate([weight_real, weight_imag], axis=1)
    right = jnp.concatenate(
        [jnp.concatenate([cos_v, sin_v], axis=2), jnp.concatenate([-sin_v, cos_v], axis=2)], axis=1
    )
    image = jnp.einsum("ikx,iky->ixy", left, right, precision=HIGH)
    image = image.reshape(count, NS, 2, NS)
    table = block_matrix(*phase_table(NS, NS, NS, -1.0))
    half = jnp.einsum("ixcy,ocyq->ixoq", image, table, precision=HIGHEST)
    full = jnp.einsum("ocpx,ixcq->iopq", table, half, precision=HIGHEST)
    return (full / (NS * NS)).astype(jnp.bfloat16)


def slot_targets(owners, tile_count, capacity):
    onehot = (owners[:, None] == jnp.arange(tile_count)[None, :]).astype(jnp.int32)
    before = jnp.cumsum(onehot, axis=0) - onehot
    slot_rank = jnp.sum(before * onehot, axis=1)
    return owners * capacity + slot_rank


def place_windows(windows, col_hi, col_lo, col_blocks):
    slots = windows.shape[0]
    wide = jnp.arange(2 * NS)
    shift = (wide[None, None, :] == col_lo[:, None, None] + jnp.arange(NS)[None, :, None])
    shifted = jnp.einsum(
        "scpq,sqw->scpw", windows, shift.astype(jnp.bfloat16), preferred_element_type=jnp.float32
    ).astype(jnp.bfloat16)
    shifted = shifted.reshape(slots, 2, NS, 2, NS)
    hit = jnp.arange(col_blocks)[:, None, None] == col_hi[None, :, None] + jnp.arange(2)[None, None, :]
    grid = jnp.einsum(
        "bsk,scpka->cpba", hit.astype(jnp.bfloat16), shifted, preferred_element_type=jnp.float32
    )
    return grid.reshape(2, NS, col_blocks * NS)


def factor_lengths(length):
    outer_len = 2 ** ((length.bit_length() - 1) // 2)
    return (outer_len, length // outer_len)


def transform_rows(grid):
    rows = grid.shape[1]
    outer_len, inner_len = factor_lengths(G)
    split = grid.reshape(2, rows, inner_len, outer_len)
    first = block_matrix(*phase_table(inner_len, inner_len, inner_len, 1.0))
    section = jnp.einsum("opba,Pobc->Pcpa", split, first, precision=HIGH)
    twiddle_real, twiddle_imag = phase_table(inner_len, outer_len, G, 1.0)
    twiddle_real = twiddle_real[:, None, :]
    twiddle_imag = twiddle_imag[:, None, :]
    turned_real = section[0] * twiddle_real - section[1] * twiddle_imag
    turned_imag = section[0] * twiddle_imag + section[1] * twiddle_real
    turned = jnp.stack([turned_real, turned_imag])
    second = block_matrix(*phase_table(outer_len, outer_len, outer_len, 1.0))
    return jnp.einsum("Ocpa,POad->dcPp", turned, second, precision=HIGH)


def transform_cols(turned):
    outer_len, inner_len = factor_lengths(G)
    first = block_matrix(*phase_table(inner_len, inner_len, inner_len, 1.0))
    section = jnp.einsum("bmoa,Pobc->Pcma", turned, first, precision=HIGH)
    twiddle_real, twiddle_imag = phase_table(inner_len, outer_len, G, 1.0)
    twiddle_real = twiddle_real[:, None, :]
    twiddle_imag = twiddle_imag[:, None, :]
    turned_real = section[0] * twiddle_real - section[1] * twiddle_imag
    turned_imag = section[0] * twiddle_imag + section[1] * twiddle_real
    second_real, second_imag = phase_table(outer_len, outer_len, outer_len, 1.0)
    second = jnp.stack([second_real, -second_imag])
    stacked = jnp.stack([turned_real, turned_imag])
    final = jnp.einsum("ocma,oad->mdc", stacked, second, precision=HIGH)
    return final.reshape(final.shape[0], G)


def per_device(samples, uv_coords, block_owner, placement_map, block_count):
    chan_count = lax.axis_size("chan")
    tile_count = lax.axis_size("tile")
    blocks = samples.shape[1]
    channels = samples.shape[2]
    steps_time = samples.shape[-1]
    group_blocks = blocks * chan_count
    capacity = max(2, 2 * group_blocks // tile_count)
    band_rows = G // tile_count
    live_mask = (jnp.arange(blocks) < block_count.reshape(())).astype(jnp.float32)
    masked = samples[0] * live_mask[:, None, None, None]
    owners = block_owner[0, :, 0]
    cols = placement_map[0, :, 1]
    meta = jnp.stack([owners, cols // NS, cols % NS], axis=1).astype(jnp.float32)
    meta = jnp.pad(meta, ((0, 0), (0, steps_time - 3)))
    meta = jnp.broadcast_to(meta[:, None, None, :], (blocks, channels, 1, steps_time))
    payload = jnp.concatenate([masked, uv_coords[0], meta], axis=2)
    arrived = lax.all_to_all(payload, "chan", split_axis=1, concat_axis=0, tiled=True)
    arrived = arrived.reshape(group_blocks, 5, steps_time)
    formed = form_subgrids(arrived[:, 0:2], arrived[:, 2:4])
    cell_count = 2 * NS * NS
    group_meta = arrived[:, 4, 0:META].astype(jnp.bfloat16)
    arrived = jnp.concatenate([formed.reshape(group_blocks, cell_count), group_meta], axis=1)
    group_owners = group_meta[:, 0].astype(jnp.int32)
    target = slot_targets(group_owners, tile_count, capacity)
    slot_count = tile_count * capacity
    pick = (jnp.arange(slot_count)[:, None] == target[None, :]).astype(jnp.bfloat16)
    outgoing = jnp.dot(pick, arrived, preferred_element_type=jnp.float32).astype(jnp.bfloat16)
    incoming = lax.all_to_all(outgoing, "tile", split_axis=0, concat_axis=0, tiled=True)
    windows = incoming[:, :cell_count].reshape(slot_count, 2, NS, NS)
    col_hi = incoming[:, cell_count + 1].astype(jnp.int32)
    col_lo = incoming[:, cell_count + 2].astype(jnp.int32)
    tile_grid = place_windows(windows, col_hi, col_lo, G // NS)
    half = transform_rows(tile_grid)
    half = half.reshape(tile_count, G // tile_count, 2, band_rows).astype(jnp.bfloat16)
    turned = lax.all_to_all(half, "tile", split_axis=0, concat_axis=0, tiled=True)
    dirty_image = transform_cols(turned.astype(jnp.float32)) / G
    return dirty_image[None]


def solution(mesh):
    in_specs = (
        P("tile", "chan", None, None, None),
        P("tile", "chan", None, None, None),
        P("tile", "chan", None),
        P("tile", "chan", None),
        P("tile", "chan"),
    )
    out_specs = P("chan", "tile", None)
    return jax.shard_map(
        per_device, mesh=mesh, in_specs=in_specs, out_specs=out_specs, check_vma=False
    )
```

```python
import math

import jax
import jax.numpy as jnp
from jax import lax
from jax.sharding import PartitionSpec as P

G = 2048
NS = 32
META = 128
HIGH = lax.Precision.HIGH
HIGHEST = lax.Precision.HIGHEST


def phase_table(row_count, col_count, length, sign):
    index = jnp.arange(row_count)[:, None] * jnp.arange(col_count)[None, :] % length
    angle = sign * 2.0 * math.pi / length * index.astype(jnp.float32)
    return (jnp.cos(angle), jnp.sin(angle))


def block_matrix(real, imag):
    return jnp.stack([jnp.stack([real, -imag]), jnp.stack([imag, real])])


def offset_phase(coord):
    factor = 2.0 * math.pi / NS
    coarse = (8.0 * jnp.arange(4) - NS / 2.0).astype(jnp.float32)
    fine = jnp.arange(8).astype(jnp.float32)
    angle_c = coord[..., None] * coarse * factor
    angle_f = coord[..., None] * fine * factor
    cos_c, sin_c = jnp.cos(angle_c)[..., :, None], jnp.sin(angle_c)[..., :, None]
    cos_f, sin_f = jnp.cos(angle_f)[..., None, :], jnp.sin(angle_f)[..., None, :]
    real = cos_c * cos_f - sin_c * sin_f
    imag = sin_c * cos_f + cos_c * sin_f
    shape = coord.shape + (NS,)
    return real.reshape(shape), imag.reshape(shape)


def form_subgrids(masked, coords):
    count = masked.shape[0]
    cos_u, sin_u = offset_phase(coords[:, 0])
    cos_v, sin_v = offset_phase(coords[:, 1])
    vis_real = masked[:, 0, :, None]
    vis_imag = masked[:, 1, :, None]
    weight_real = vis_real * cos_u - vis_imag * sin_u
    weight_imag = vis_real * sin_u + vis_imag * cos_u
    table_real, table_imag = phase_table(NS, NS, NS, -1.0)
    table = jnp.stack(
        [
            jnp.concatenate([table_real, table_imag], axis=1),
            jnp.concatenate([-table_imag, table_real], axis=1),
        ]
    )
    row_side = jnp.einsum(
        "ikcx,cxn->ikn", jnp.stack([weight_real, weight_imag], axis=2), table, precision=HIGH
    )
    col_side = jnp.einsum(
        "ikcx,cxn->ikn", jnp.stack([cos_v, sin_v], axis=2), table, precision=HIGH
    )
    left = jnp.concatenate([row_side[:, :, :NS], row_side[:, :, NS:]], axis=1)
    right = jnp.concatenate(
        [col_side, jnp.concatenate([-col_side[:, :, NS:], col_side[:, :, :NS]], axis=2)], axis=1
    )
    full = jnp.einsum("ikp,ikn->ipn", left, right, precision=HIGH)
    return (full.reshape(count, NS, 2, NS) / (NS * NS)).astype(jnp.bfloat16)


def slot_targets(owners, tile_count, capacity):
    onehot = (owners[:, None] == jnp.arange(tile_count)[None, :]).astype(jnp.int32)
    before = jnp.cumsum(onehot, axis=0) - onehot
    slot_rank = jnp.sum(before * onehot, axis=1)
    return owners * capacity + slot_rank


def place_windows(windows, col_hi, col_lo, col_blocks):
    slots = windows.shape[0]
    wide = jnp.arange(2 * NS)
    shift = (wide[None, None, :] == col_lo[:, None, None] + jnp.arange(NS)[None, :, None])
    shifted = jnp.einsum(
        "scpq,sqw->scpw", windows, shift.astype(jnp.bfloat16), preferred_element_type=jnp.float32
    ).astype(jnp.bfloat16)
    shifted = shifted.reshape(slots, 2, NS, 2, NS)
    hit = jnp.arange(col_blocks)[:, None, None] == col_hi[None, :, None] + jnp.arange(2)[None, None, :]
    grid = jnp.einsum(
        "bsk,scpka->cpba", hit.astype(jnp.bfloat16), shifted, preferred_element_type=jnp.float32
    )
    return grid.reshape(2, NS, col_blocks * NS)


def factor_lengths(length):
    outer_len = 2 ** ((length.bit_length() - 1) // 2)
    return (outer_len, length // outer_len)


def transform_rows(grid):
    rows = grid.shape[1]
    outer_len, inner_len = factor_lengths(G)
    split = grid.reshape(2, rows, inner_len, outer_len)
    first = block_matrix(*phase_table(inner_len, inner_len, inner_len, 1.0))
    section = jnp.einsum("opba,Pobc->Pcpa", split, first, precision=HIGH)
    twiddle_real, twiddle_imag = phase_table(inner_len, outer_len, G, 1.0)
    twiddle_real = twiddle_real[:, None, :]
    twiddle_imag = twiddle_imag[:, None, :]
    turned_real = section[0] * twiddle_real - section[1] * twiddle_imag
    turned_imag = section[0] * twiddle_imag + section[1] * twiddle_real
    turned = jnp.stack([turned_real, turned_imag])
    second = block_matrix(*phase_table(outer_len, outer_len, outer_len, 1.0))
    return jnp.einsum("Ocpa,POad->dcPp", turned, second, precision=HIGH)


def transform_cols(turned):
    outer_len, inner_len = factor_lengths(G)
    first = block_matrix(*phase_table(inner_len, inner_len, inner_len, 1.0))
    section = jnp.einsum("bmoa,Pobc->Pcma", turned, first, precision=HIGH)
    twiddle_real, twiddle_imag = phase_table(inner_len, outer_len, G, 1.0)
    twiddle_real = twiddle_real[:, None, :]
    twiddle_imag = twiddle_imag[:, None, :]
    turned_real = section[0] * twiddle_real - section[1] * twiddle_imag
    turned_imag = section[0] * twiddle_imag + section[1] * twiddle_real
    second_real, second_imag = phase_table(outer_len, outer_len, outer_len, 1.0)
    second = jnp.stack([second_real, -second_imag])
    stacked = jnp.stack([turned_real, turned_imag])
    final = jnp.einsum("ocma,oad->mdc", stacked, second, precision=HIGH)
    return final.reshape(final.shape[0], G)


def per_device(samples, uv_coords, block_owner, placement_map, block_count):
    chan_count = lax.axis_size("chan")
    tile_count = lax.axis_size("tile")
    blocks = samples.shape[1]
    channels = samples.shape[2]
    steps_time = samples.shape[-1]
    group_blocks = blocks * chan_count
    capacity = max(2, 2 * group_blocks // tile_count)
    band_rows = G // tile_count
    live_mask = (jnp.arange(blocks) < block_count.reshape(())).astype(jnp.float32)
    masked = samples[0] * live_mask[:, None, None, None]
    owners = block_owner[0, :, 0]
    cols = placement_map[0, :, 1]
    meta = jnp.stack([owners, cols // NS, cols % NS], axis=1).astype(jnp.float32)
    meta = jnp.pad(meta, ((0, 0), (0, steps_time - 3)))
    meta = jnp.broadcast_to(meta[:, None, None, :], (blocks, channels, 1, steps_time))
    payload = jnp.concatenate([masked, uv_coords[0], meta], axis=2)
    arrived = lax.all_to_all(payload, "chan", split_axis=1, concat_axis=0, tiled=True)
    arrived = arrived.reshape(group_blocks, 5, steps_time)
    formed = form_subgrids(arrived[:, 0:2], arrived[:, 2:4])
    cell_count = 2 * NS * NS
    group_meta = arrived[:, 4, 0:META].astype(jnp.bfloat16)
    arrived = jnp.concatenate([formed.reshape(group_blocks, cell_count), group_meta], axis=1)
    group_owners = group_meta[:, 0].astype(jnp.int32)
    target = slot_targets(group_owners, tile_count, capacity)
    slot_count = tile_count * capacity
    pick = (jnp.arange(slot_count)[:, None] == target[None, :]).astype(jnp.bfloat16)
    outgoing = jnp.dot(pick, arrived, preferred_element_type=jnp.float32).astype(jnp.bfloat16)
    incoming = lax.all_to_all(outgoing, "tile", split_axis=0, concat_axis=0, tiled=True)
    windows = incoming[:, :cell_count].reshape(slot_count, NS, 2, NS).transpose(0, 2, 1, 3)
    col_hi = incoming[:, cell_count + 1].astype(jnp.int32)
    col_lo = incoming[:, cell_count + 2].astype(jnp.int32)
    tile_grid = place_windows(windows, col_hi, col_lo, G // NS)
    half = transform_rows(tile_grid)
    half = half.reshape(tile_count, G // tile_count, 2, band_rows).astype(jnp.bfloat16)
    turned = lax.all_to_all(half, "tile", split_axis=0, concat_axis=0, tiled=True)
    dirty_image = transform_cols(turned.astype(jnp.float32)) / G
    return dirty_image[None]


def solution(mesh):
    in_specs = (
        P("tile", "chan", None, None, None),
        P("tile", "chan", None, None, None),
        P("tile", "chan", None),
        P("tile", "chan", None),
        P("tile", "chan"),
    )
    out_specs = P("chan", "tile", None)
    return jax.shard_map(
        per_device, mesh=mesh, in_specs=in_specs, out_specs=out_specs, check_vma=False
    )
```

```python
import math

import jax
import jax.numpy as jnp
from jax import lax
from jax.experimental import pallas as pl
from jax.experimental.pallas import tpu as pltpu
from jax.sharding import PartitionSpec as P

G = 2048
NS = 32
META = 128
HIGH = lax.Precision.HIGH
HIGHEST = lax.Precision.HIGHEST


def phase_table(row_count, col_count, length, sign):
    index = jnp.arange(row_count)[:, None] * jnp.arange(col_count)[None, :] % length
    angle = sign * 2.0 * math.pi / length * index.astype(jnp.float32)
    return (jnp.cos(angle), jnp.sin(angle))


def block_matrix(real, imag):
    return jnp.stack([jnp.stack([real, -imag]), jnp.stack([imag, real])])


def offset_phase(coord):
    factor = 2.0 * math.pi / NS
    coarse = (8.0 * jnp.arange(4) - NS / 2.0).astype(jnp.float32)
    fine = jnp.arange(8).astype(jnp.float32)
    angle_c = coord[..., None] * coarse * factor
    angle_f = coord[..., None] * fine * factor
    cos_c, sin_c = jnp.cos(angle_c)[..., :, None], jnp.sin(angle_c)[..., :, None]
    cos_f, sin_f = jnp.cos(angle_f)[..., None, :], jnp.sin(angle_f)[..., None, :]
    real = cos_c * cos_f - sin_c * sin_f
    imag = sin_c * cos_f + cos_c * sin_f
    shape = coord.shape + (NS,)
    return real.reshape(shape), imag.reshape(shape)


def form_subgrids(masked, coords):
    count = masked.shape[0]
    cos_u, sin_u = offset_phase(coords[:, 0])
    cos_v, sin_v = offset_phase(coords[:, 1])
    vis_real = masked[:, 0, :, None]
    vis_imag = masked[:, 1, :, None]
    weight_real = vis_real * cos_u - vis_imag * sin_u
    weight_imag = vis_real * sin_u + vis_imag * cos_u
    table_real, table_imag = phase_table(NS, NS, NS, -1.0)
    table = jnp.stack(
        [
            jnp.concatenate([table_real, table_imag], axis=1),
            jnp.concatenate([-table_imag, table_real], axis=1),
        ]
    )
    row_side = jnp.einsum(
        "ikcx,cxn->ikn", jnp.stack([weight_real, weight_imag], axis=2), table, precision=HIGH
    )
    col_side = jnp.einsum(
        "ikcx,cxn->ikn", jnp.stack([cos_v, sin_v], axis=2), table, precision=HIGH
    )
    left = jnp.concatenate([col_side[:, :, :NS], col_side[:, :, NS:]], axis=1)
    right = jnp.concatenate(
        [row_side, jnp.concatenate([-row_side[:, :, NS:], row_side[:, :, :NS]], axis=2)], axis=1
    )
    full = jnp.einsum("ikq,ikn->iqn", left, right, precision=HIGH)
    return (full.reshape(count, NS, 2, NS) / (NS * NS)).astype(jnp.bfloat16)


def slot_targets(owners, tile_count, capacity):
    onehot = (owners[:, None] == jnp.arange(tile_count)[None, :]).astype(jnp.int32)
    before = jnp.cumsum(onehot, axis=0) - onehot
    slot_rank = jnp.sum(before * onehot, axis=1)
    return owners * capacity + slot_rank


def place_kernel(cols_ref, windows_ref, grid_ref):
    grid_ref[...] = jnp.zeros(grid_ref.shape, grid_ref.dtype)
    width = windows_ref.shape[1]

    def add_slot(slot, carry):
        start = cols_ref[slot]
        grid_ref[pl.ds(start, width), :] += windows_ref[slot].astype(jnp.float32)
        return carry

    lax.fori_loop(0, windows_ref.shape[0], add_slot, 0, unroll=8)


def place_slots(cols, windows):
    slots, width, lanes = windows.shape
    return pl.pallas_call(
        place_kernel,
        out_shape=jax.ShapeDtypeStruct((G, lanes), jnp.float32),
        grid_spec=pltpu.PrefetchScalarGridSpec(
            num_scalar_prefetch=1,
            grid=(1,),
            in_specs=[pl.BlockSpec((slots, width, lanes), lambda i, c: (0, 0, 0))],
            out_specs=pl.BlockSpec((G, lanes), lambda i, c: (0, 0)),
        ),
        cost_estimate=pl.CostEstimate(
            flops=slots * width * lanes, transcendentals=0, bytes_accessed=slots * width * lanes * 2 + G * lanes * 4
        ),
    )(cols, windows)


def factor_lengths(length):
    outer_len = 2 ** ((length.bit_length() - 1) // 2)
    return (outer_len, length // outer_len)


def transform_rows(grid):
    outer_len, inner_len = factor_lengths(G)
    first = block_matrix(*phase_table(inner_len, inner_len, inner_len, 1.0))
    section = jnp.einsum("baop,Pobc->caPp", grid, first, precision=HIGH)
    twiddle_real, twiddle_imag = phase_table(inner_len, outer_len, G, 1.0)
    twiddle_real = twiddle_real[:, :, None]
    twiddle_imag = twiddle_imag[:, :, None]
    section_real, section_imag = section[:, :, 0], section[:, :, 1]
    turned_real = section_real * twiddle_real - section_imag * twiddle_imag
    turned_imag = section_real * twiddle_imag + section_imag * twiddle_real
    turned = jnp.stack([turned_real, turned_imag], axis=2)
    second = block_matrix(*phase_table(outer_len, outer_len, outer_len, 1.0))
    return jnp.einsum("caOp,POad->dcPp", turned, second, precision=HIGH)


def transform_cols(turned):
    outer_len, inner_len = factor_lengths(G)
    first = block_matrix(*phase_table(inner_len, inner_len, inner_len, 1.0))
    section = jnp.einsum("bmoa,Pobc->Pcma", turned, first, precision=HIGH)
    twiddle_real, twiddle_imag = phase_table(inner_len, outer_len, G, 1.0)
    twiddle_real = twiddle_real[:, None, :]
    twiddle_imag = twiddle_imag[:, None, :]
    turned_real = section[0] * twiddle_real - section[1] * twiddle_imag
    turned_imag = section[0] * twiddle_imag + section[1] * twiddle_real
    second_real, second_imag = phase_table(outer_len, outer_len, outer_len, 1.0)
    second = jnp.stack([second_real, -second_imag]) / G
    stacked = jnp.stack([turned_real, turned_imag])
    final = jnp.einsum("ocma,oad->mdc", stacked, second, precision=HIGH)
    return final.reshape(final.shape[0], G)


def per_device(samples, uv_coords, block_owner, placement_map, block_count):
    chan_count = lax.axis_size("chan")
    tile_count = lax.axis_size("tile")
    blocks = samples.shape[1]
    channels = samples.shape[2]
    steps_time = samples.shape[-1]
    group_blocks = blocks * chan_count
    capacity = max(2, 2 * group_blocks // tile_count)
    band_rows = G // tile_count
    live_mask = (jnp.arange(blocks) < block_count.reshape(())).astype(jnp.float32)
    masked = samples[0] * live_mask[:, None, None, None]
    owners = block_owner[0, :, 0]
    cols = placement_map[0, :, 1]
    meta = jnp.stack([owners, cols // NS, cols % NS], axis=1).astype(jnp.float32)
    meta = jnp.pad(meta, ((0, 0), (0, steps_time - 3)))
    meta = jnp.broadcast_to(meta[:, None, None, :], (blocks, channels, 1, steps_time))
    payload = jnp.concatenate([masked, uv_coords[0], meta], axis=2)
    arrived = lax.all_to_all(payload, "chan", split_axis=1, concat_axis=0, tiled=True)
    arrived = arrived.reshape(group_blocks, 5, steps_time)
    formed = form_subgrids(arrived[:, 0:2], arrived[:, 2:4])
    cell_count = 2 * NS * NS
    group_meta = arrived[:, 4, 0:META].astype(jnp.bfloat16)
    arrived = jnp.concatenate([formed.reshape(group_blocks, cell_count), group_meta], axis=1)
    group_owners = group_meta[:, 0].astype(jnp.int32)
    target = slot_targets(group_owners, tile_count, capacity)
    slot_count = tile_count * capacity
    pick = (jnp.arange(slot_count)[:, None] == target[None, :]).astype(jnp.bfloat16)
    outgoing = jnp.dot(pick, arrived, preferred_element_type=jnp.float32).astype(jnp.bfloat16)
    incoming = lax.all_to_all(outgoing, "tile", split_axis=0, concat_axis=0, tiled=True)
    windows = incoming[:, :cell_count].reshape(slot_count, NS, 2 * NS)
    col_hi = incoming[:, cell_count + 1].astype(jnp.int32)
    col_lo = incoming[:, cell_count + 2].astype(jnp.int32)
    cols = jnp.clip(col_hi * NS + col_lo, 0, G - NS)
    tile_grid = place_slots(cols, windows)
    half = transform_rows(tile_grid.reshape(G // NS, NS, 2, band_rows))
    half = half.reshape(tile_count, G // tile_count, 2, band_rows).astype(jnp.bfloat16)
    turned = lax.all_to_all(half, "tile", split_axis=0, concat_axis=0, tiled=True)
    dirty_image = transform_cols(turned.astype(jnp.float32))
    return dirty_image[None]


def solution(mesh):
    in_specs = (
        P("tile", "chan", None, None, None),
        P("tile", "chan", None, None, None),
        P("tile", "chan", None),
        P("tile", "chan", None),
        P("tile", "chan"),
    )
    out_specs = P("chan", "tile", None)
    return jax.shard_map(
        per_device, mesh=mesh, in_specs=in_specs, out_specs=out_specs, check_vma=False
    )
```

```python
import math

import jax
import jax.numpy as jnp
from jax import lax
from jax.experimental import pallas as pl
from jax.experimental.pallas import tpu as pltpu
from jax.sharding import PartitionSpec as P

G = 2048
NS = 32
META = 128
HIGH = lax.Precision.HIGH
HIGHEST = lax.Precision.HIGHEST


def phase_table(row_count, col_count, length, sign):
    index = jnp.arange(row_count)[:, None] * jnp.arange(col_count)[None, :] % length
    angle = sign * 2.0 * math.pi / length * index.astype(jnp.float32)
    return (jnp.cos(angle), jnp.sin(angle))


def block_matrix(real, imag):
    return jnp.stack([jnp.stack([real, -imag]), jnp.stack([imag, real])])


def offset_phase(coord):
    factor = 2.0 * math.pi / NS
    coarse = (8.0 * jnp.arange(4) - NS / 2.0).astype(jnp.float32)
    fine = jnp.arange(8).astype(jnp.float32)
    angle_c = coord[..., None] * coarse * factor
    angle_f = coord[..., None] * fine * factor
    cos_c, sin_c = jnp.cos(angle_c)[..., :, None], jnp.sin(angle_c)[..., :, None]
    cos_f, sin_f = jnp.cos(angle_f)[..., None, :], jnp.sin(angle_f)[..., None, :]
    real = cos_c * cos_f - sin_c * sin_f
    imag = sin_c * cos_f + cos_c * sin_f
    shape = coord.shape + (NS,)
    return real.reshape(shape), imag.reshape(shape)


def form_subgrids(masked, coords):
    count = masked.shape[0]
    cos_u, sin_u = offset_phase(coords[:, 0])
    cos_v, sin_v = offset_phase(coords[:, 1])
    vis_real = masked[:, 0, :, None]
    vis_imag = masked[:, 1, :, None]
    weight_real = vis_real * cos_u - vis_imag * sin_u
    weight_imag = vis_real * sin_u + vis_imag * cos_u
    table_real, table_imag = phase_table(NS, NS, NS, -1.0)
    table = jnp.stack(
        [
            jnp.concatenate([table_real, table_imag], axis=1),
            jnp.concatenate([-table_imag, table_real], axis=1),
        ]
    )
    row_side = jnp.einsum(
        "ikcx,cxn->ikn", jnp.stack([weight_real, weight_imag], axis=2), table, precision=HIGH
    )
    col_side = jnp.einsum(
        "ikcx,cxn->ikn", jnp.stack([cos_v, sin_v], axis=2), table, precision=HIGH
    )
    left = jnp.concatenate([col_side[:, :, :NS], col_side[:, :, NS:]], axis=1)
    right = jnp.concatenate(
        [row_side, jnp.concatenate([-row_side[:, :, NS:], row_side[:, :, :NS]], axis=2)], axis=1
    )
    full = jnp.einsum("ikq,ikn->iqn", left, right, precision=HIGH)
    return (full.reshape(count, NS, 2, NS) / (NS * NS)).astype(jnp.bfloat16)


def slot_targets(owners, tile_count, capacity):
    onehot = (owners[:, None] == jnp.arange(tile_count)[None, :]).astype(jnp.int32)
    before = jnp.cumsum(onehot, axis=0) - onehot
    slot_rank = jnp.sum(before * onehot, axis=1)
    return owners * capacity + slot_rank


def place_kernel(cols_ref, tiles_ref, grid_ref):
    grid_ref[...] = jnp.zeros(grid_ref.shape, grid_ref.dtype)
    width = 2 * NS

    def add_source(source, carry):
        for rank in range(2):
            start = cols_ref[2 * source + rank]
            window = tiles_ref[source, 0:NS, rank * width:(rank + 1) * width]
            grid_ref[pl.ds(start, NS), :] += window.astype(jnp.float32)
        return carry

    lax.fori_loop(0, tiles_ref.shape[0], add_source, 0, unroll=4)


def place_slots(cols, tiles):
    sources, rows, lanes = tiles.shape
    return pl.pallas_call(
        place_kernel,
        out_shape=jax.ShapeDtypeStruct((G, lanes // 2), jnp.float32),
        grid_spec=pltpu.PrefetchScalarGridSpec(
            num_scalar_prefetch=1,
            grid=(1,),
            in_specs=[pl.BlockSpec((sources, rows, lanes), lambda i, c: (0, 0, 0))],
            out_specs=pl.BlockSpec((G, lanes // 2), lambda i, c: (0, 0)),
        ),
        cost_estimate=pl.CostEstimate(
            flops=sources * rows * lanes, transcendentals=0, bytes_accessed=sources * rows * lanes * 2 + G * lanes * 2
        ),
    )(cols, tiles)


def times_i(x):
    half = x.shape[-1] // 2
    return jnp.concatenate([-x[..., half:], x[..., :half]], axis=-1)


def factor_lengths(length):
    outer_len = 2 ** ((length.bit_length() - 1) // 2)
    return (outer_len, length // outer_len)


def transform_rows(grid):
    outer_len, inner_len = factor_lengths(G)
    first_real, first_imag = phase_table(inner_len, inner_len, inner_len, 1.0)
    section = jnp.einsum("cb,ban->can", first_real, grid, precision=HIGH) + jnp.einsum(
        "cb,ban->can", first_imag, times_i(grid), precision=HIGH
    )
    twiddle_real, twiddle_imag = phase_table(inner_len, outer_len, G, 1.0)
    turned = section * twiddle_real[:, :, None] + times_i(section) * twiddle_imag[:, :, None]
    second_real, second_imag = phase_table(outer_len, outer_len, outer_len, 1.0)
    return jnp.einsum("da,can->dcn", second_real, turned, precision=HIGH) + jnp.einsum(
        "da,can->dcn", second_imag, times_i(turned), precision=HIGH
    )


def transform_cols(turned):
    outer_len, inner_len = factor_lengths(G)
    first = block_matrix(*phase_table(inner_len, inner_len, inner_len, 1.0))
    section = jnp.einsum("bmoa,Pobc->Pcma", turned, first, precision=HIGH)
    twiddle_real, twiddle_imag = phase_table(inner_len, outer_len, G, 1.0)
    twiddle_real = twiddle_real[:, None, :]
    twiddle_imag = twiddle_imag[:, None, :]
    turned_real = section[0] * twiddle_real - section[1] * twiddle_imag
    turned_imag = section[0] * twiddle_imag + section[1] * twiddle_real
    second_real, second_imag = phase_table(outer_len, outer_len, outer_len, 1.0)
    second = jnp.stack([second_real, -second_imag])
    stacked = jnp.stack([turned_real, turned_imag])
    final = jnp.einsum("ocma,oad->mdc", stacked, second, precision=HIGH)
    return final.reshape(final.shape[0], G)


def per_device(samples, uv_coords, block_owner, placement_map, block_count):
    chan_count = lax.axis_size("chan")
    tile_count = lax.axis_size("tile")
    blocks = samples.shape[1]
    channels = samples.shape[2]
    steps_time = samples.shape[-1]
    group_blocks = blocks * chan_count
    capacity = max(2, 2 * group_blocks // tile_count)
    band_rows = G // tile_count
    live_mask = (jnp.arange(blocks) < block_count.reshape(())).astype(jnp.float32)
    masked = samples[0] * live_mask[:, None, None, None]
    owners = block_owner[0, :, 0]
    cols = placement_map[0, :, 1]
    meta = jnp.stack([owners, cols // NS, cols % NS], axis=1).astype(jnp.float32)
    meta = jnp.pad(meta, ((0, 0), (0, steps_time - 3)))
    meta = jnp.broadcast_to(meta[:, None, None, :], (blocks, channels, 1, steps_time))
    payload = jnp.concatenate([masked, uv_coords[0], meta], axis=2)
    arrived = lax.all_to_all(payload, "chan", split_axis=1, concat_axis=0, tiled=True)
    arrived = arrived.reshape(group_blocks, 5, steps_time)
    formed = form_subgrids(arrived[:, 0:2], arrived[:, 2:4])
    cell_count = 2 * NS * NS
    group_meta = arrived[:, 4, 0:META].astype(jnp.bfloat16)
    arrived = jnp.concatenate([formed.reshape(group_blocks, cell_count), group_meta], axis=1)
    group_owners = group_meta[:, 0].astype(jnp.int32)
    target = slot_targets(group_owners, tile_count, capacity)
    slot_count = tile_count * capacity
    pick = (jnp.arange(slot_count)[:, None] == target[None, :]).astype(jnp.bfloat16)
    outgoing = jnp.dot(pick, arrived, preferred_element_type=jnp.float32).astype(jnp.bfloat16)
    lanes = 2 * NS
    windows = outgoing[:, :cell_count].reshape(tile_count, capacity, NS, lanes)
    windows = windows.transpose(0, 2, 1, 3).reshape(tile_count, NS, capacity * lanes)
    where_to = outgoing[:, cell_count + 1:cell_count + 3].reshape(tile_count, capacity, 2)
    where_to = jnp.pad(where_to, ((0, 0), (0, 0), (0, lanes - 2))).reshape(tile_count, 1, capacity * lanes)
    tiles = jnp.concatenate([windows, where_to], axis=1)
    incoming = lax.all_to_all(tiles, "tile", split_axis=0, concat_axis=0, tiled=True)
    places = incoming[:, NS].reshape(tile_count, capacity, lanes)[:, :, 0:2].astype(jnp.int32)
    cols = jnp.clip(places[:, :, 0] * NS + places[:, :, 1], 0, G - NS).reshape(slot_count)
    tile_grid = place_slots(cols, incoming)
    half = transform_rows(tile_grid.reshape(G // NS, NS, lanes))
    half = half.reshape(tile_count, G // tile_count, 2, band_rows).astype(jnp.bfloat16)
    turned = lax.all_to_all(half, "tile", split_axis=0, concat_axis=0, tiled=True)
    dirty_image = transform_cols(turned.astype(jnp.float32)) / G
    return dirty_image[None]


def solution(mesh):
    in_specs = (
        P("tile", "chan", None, None, None),
        P("tile", "chan", None, None, None),
        P("tile", "chan", None),
        P("tile", "chan", None),
        P("tile", "chan"),
    )
    out_specs = P("chan", "tile", None)
    return jax.shard_map(
        per_device, mesh=mesh, in_specs=in_specs, out_specs=out_specs, check_vma=False
    )
```

```python
import math

import jax
import jax.numpy as jnp
from jax import lax
from jax.sharding import PartitionSpec as P

G = 2048
NS = 32
META = 128
HIGH = lax.Precision.HIGH
HIGHEST = lax.Precision.HIGHEST


def phase_table(row_count, col_count, length, sign):
    index = jnp.arange(row_count)[:, None] * jnp.arange(col_count)[None, :] % length
    angle = sign * 2.0 * math.pi / length * index.astype(jnp.float32)
    return (jnp.cos(angle), jnp.sin(angle))


def block_matrix(real, imag):
    return jnp.stack([jnp.stack([real, -imag]), jnp.stack([imag, real])])


def offset_phase(coord):
    factor = 2.0 * math.pi / NS
    coarse = (8.0 * jnp.arange(4) - NS / 2.0).astype(jnp.float32)
    fine = jnp.arange(8).astype(jnp.float32)
    angle_c = coord[..., None] * coarse * factor
    angle_f = coord[..., None] * fine * factor
    cos_c, sin_c = jnp.cos(angle_c)[..., :, None], jnp.sin(angle_c)[..., :, None]
    cos_f, sin_f = jnp.cos(angle_f)[..., None, :], jnp.sin(angle_f)[..., None, :]
    real = cos_c * cos_f - sin_c * sin_f
    imag = sin_c * cos_f + cos_c * sin_f
    shape = coord.shape + (NS,)
    return real.reshape(shape), imag.reshape(shape)


def form_subgrids(masked, coords):
    count = masked.shape[0]
    cos_u, sin_u = offset_phase(coords[:, 0])
    cos_v, sin_v = offset_phase(coords[:, 1])
    vis_real = masked[:, 0, :, None]
    vis_imag = masked[:, 1, :, None]
    weight_real = vis_real * cos_u - vis_imag * sin_u
    weight_imag = vis_real * sin_u + vis_imag * cos_u
    table_real, table_imag = phase_table(NS, NS, NS, -1.0)
    table = jnp.stack(
        [
            jnp.concatenate([table_real, table_imag], axis=1),
            jnp.concatenate([-table_imag, table_real], axis=1),
        ]
    )
    row_side = jnp.einsum(
        "ikcx,cxn->ikn", jnp.stack([weight_real, weight_imag], axis=2), table, precision=HIGH
    )
    col_side = jnp.einsum(
        "ikcx,cxn->ikn", jnp.stack([cos_v, sin_v], axis=2), table, precision=HIGH
    )
    left = jnp.concatenate([row_side[:, :, :NS], row_side[:, :, NS:]], axis=1)
    right = jnp.concatenate(
        [col_side, jnp.concatenate([-col_side[:, :, NS:], col_side[:, :, :NS]], axis=2)], axis=1
    )
    full = jnp.einsum("ikp,ikn->ipn", left, right, precision=HIGH)
    return (full.reshape(count, NS, 2, NS) / (NS * NS)).astype(jnp.bfloat16)


def slot_targets(owners, tile_count, capacity):
    onehot = (owners[:, None] == jnp.arange(tile_count)[None, :]).astype(jnp.int32)
    before = jnp.cumsum(onehot, axis=0) - onehot
    slot_rank = jnp.sum(before * onehot, axis=1)
    return owners * capacity + slot_rank


def place_windows(windows, col_hi, col_lo, col_blocks):
    slots = windows.shape[0]
    wide = jnp.arange(2 * NS)
    shift = (wide[None, None, :] == col_lo[:, None, None] + jnp.arange(NS)[None, :, None])
    shifted = jnp.einsum(
        "scpq,sqw->scpw", windows, shift.astype(jnp.bfloat16), preferred_element_type=jnp.float32
    ).astype(jnp.bfloat16)
    shifted = shifted.reshape(slots, 2, NS, 2, NS)
    hit = jnp.arange(col_blocks)[:, None, None] == col_hi[None, :, None] + jnp.arange(2)[None, None, :]
    grid = jnp.einsum(
        "bsk,scpka->cpba", hit.astype(jnp.bfloat16), shifted, preferred_element_type=jnp.float32
    )
    return grid.reshape(2, NS, col_blocks * NS)


def factor_lengths(length):
    outer_len = 2 ** ((length.bit_length() - 1) // 2)
    return (outer_len, length // outer_len)


def transform_rows(grid):
    rows = grid.shape[1]
    outer_len, inner_len = factor_lengths(G)
    split = grid.reshape(2, rows, inner_len, outer_len)
    first = block_matrix(*phase_table(inner_len, inner_len, inner_len, 1.0))
    section = jnp.einsum("opba,Pobc->Pcpa", split, first, precision=HIGH)
    twiddle_real, twiddle_imag = phase_table(inner_len, outer_len, G, 1.0)
    twiddle_real = twiddle_real[:, None, :]
    twiddle_imag = twiddle_imag[:, None, :]
    turned_real = section[0] * twiddle_real - section[1] * twiddle_imag
    turned_imag = section[0] * twiddle_imag + section[1] * twiddle_real
    turned = jnp.stack([turned_real, turned_imag])
    second = block_matrix(*phase_table(outer_len, outer_len, outer_len, 1.0))
    return jnp.einsum("Ocpa,POad->dcPp", turned, second, precision=HIGH)


def transform_cols(turned):
    outer_len, inner_len = factor_lengths(G)
    first = block_matrix(*phase_table(inner_len, inner_len, inner_len, 1.0))
    section = jnp.einsum("bmoa,Pobc->Pcma", turned, first, precision=HIGH)
    twiddle_real, twiddle_imag = phase_table(inner_len, outer_len, G, 1.0)
    twiddle_real = twiddle_real[:, None, :]
    twiddle_imag = twiddle_imag[:, None, :]
    turned_real = section[0] * twiddle_real - section[1] * twiddle_imag
    turned_imag = section[0] * twiddle_imag + section[1] * twiddle_real
    second_real, second_imag = phase_table(outer_len, outer_len, outer_len, 1.0)
    second = jnp.stack([second_real, -second_imag]) / G
    stacked = jnp.stack([turned_real, turned_imag])
    final = jnp.einsum("ocma,oad->mdc", stacked, second, precision=HIGH)
    return final.reshape(final.shape[0], G)


def per_device(samples, uv_coords, block_owner, placement_map, block_count):
    chan_count = lax.axis_size("chan")
    tile_count = lax.axis_size("tile")
    blocks = samples.shape[1]
    channels = samples.shape[2]
    steps_time = samples.shape[-1]
    group_blocks = blocks * chan_count
    capacity = max(2, 2 * group_blocks // tile_count)
    band_rows = G // tile_count
    live_mask = (jnp.arange(blocks) < block_count.reshape(())).astype(jnp.float32)
    masked = samples[0] * live_mask[:, None, None, None]
    owners = block_owner[0, :, 0]
    cols = placement_map[0, :, 1]
    meta = jnp.stack([owners, cols], axis=1).astype(jnp.float32)
    meta = jnp.pad(meta, ((0, 0), (0, steps_time - 2)))
    meta = jnp.broadcast_to(meta[:, None, None, :], (blocks, channels, 1, steps_time))
    payload = jnp.concatenate([masked, uv_coords[0], meta], axis=2)
    arrived = lax.all_to_all(payload, "chan", split_axis=1, concat_axis=0, tiled=True)
    arrived = arrived.reshape(group_blocks, 5, steps_time)
    formed = form_subgrids(arrived[:, 0:2], arrived[:, 2:4])
    cell_count = 2 * NS * NS
    group_cols = arrived[:, 4, 1]
    col_hi = jnp.floor(group_cols / NS)
    col_lo = group_cols - NS * col_hi
    group_meta = jnp.stack([arrived[:, 4, 0], col_hi, col_lo], axis=1)
    group_meta = jnp.pad(group_meta, ((0, 0), (0, META - 3))).astype(jnp.bfloat16)
    arrived = jnp.concatenate([formed.reshape(group_blocks, cell_count), group_meta], axis=1)
    group_owners = group_meta[:, 0].astype(jnp.int32)
    target = slot_targets(group_owners, tile_count, capacity)
    slot_count = tile_count * capacity
    pick = (jnp.arange(slot_count)[:, None] == target[None, :]).astype(jnp.bfloat16)
    outgoing = jnp.dot(pick, arrived, preferred_element_type=jnp.float32).astype(jnp.bfloat16)
    incoming = lax.all_to_all(outgoing, "tile", split_axis=0, concat_axis=0, tiled=True)
    windows = incoming[:, :cell_count].reshape(slot_count, NS, 2, NS).transpose(0, 2, 1, 3)
    col_hi = incoming[:, cell_count + 1].astype(jnp.int32)
    col_lo = incoming[:, cell_count + 2].astype(jnp.int32)
    tile_grid = place_windows(windows, col_hi, col_lo, G // NS)
    half = transform_rows(tile_grid)
    half = half.reshape(tile_count, G // tile_count, 2, band_rows).astype(jnp.bfloat16)
    turned = lax.all_to_all(half, "tile", split_axis=0, concat_axis=0, tiled=True)
    dirty_image = transform_cols(turned.astype(jnp.float32))
    return dirty_image[None]


def solution(mesh):
    in_specs = (
        P("tile", "chan", None, None, None),
        P("tile", "chan", None, None, None),
        P("tile", "chan", None),
        P("tile", "chan", None),
        P("tile", "chan"),
    )
    out_specs = P("chan", "tile", None)
    return jax.shard_map(
        per_device, mesh=mesh, in_specs=in_specs, out_specs=out_specs, check_vma=False
    )
```

```python
import math

import jax
import jax.numpy as jnp
from jax import lax
from jax.sharding import PartitionSpec as P

G = 2048
NS = 32
META = 128
HIGH = lax.Precision.HIGH
HIGHEST = lax.Precision.HIGHEST


def phase_table(row_count, col_count, length, sign):
    index = jnp.arange(row_count)[:, None] * jnp.arange(col_count)[None, :] % length
    angle = sign * 2.0 * math.pi / length * index.astype(jnp.float32)
    return (jnp.cos(angle), jnp.sin(angle))


def block_matrix(real, imag):
    return jnp.stack([jnp.stack([real, -imag]), jnp.stack([imag, real])])


def complex_product(left, right):
    return (left[0] * right[0] - left[1] * right[1], left[0] * right[1] + left[1] * right[0])


def bit_select(bits, value):
    return (jnp.where(bits, value[0], 1.0), jnp.where(bits, value[1], 0.0))


def offset_phase(coord):
    theta = coord * (2.0 * math.pi / NS)
    squares = [(jnp.cos(theta)[..., None], jnp.sin(theta)[..., None])]
    for _ in range(4):
        squares.append(complex_product(squares[-1], squares[-1]))
    fine_index = jnp.arange(8)
    fine = bit_select((fine_index & 1) > 0, squares[0])
    fine = complex_product(fine, bit_select((fine_index & 2) > 0, squares[1]))
    fine = complex_product(fine, bit_select((fine_index & 4) > 0, squares[2]))
    coarse_index = jnp.arange(4)
    start = (squares[4][0], -squares[4][1])
    coarse = complex_product(start, bit_select((coarse_index & 1) > 0, squares[3]))
    coarse = complex_product(coarse, bit_select((coarse_index & 2) > 0, squares[4]))
    real = coarse[0][..., :, None] * fine[0][..., None, :] - coarse[1][..., :, None] * fine[1][..., None, :]
    imag = coarse[1][..., :, None] * fine[0][..., None, :] + coarse[0][..., :, None] * fine[1][..., None, :]
    shape = coord.shape + (NS,)
    return real.reshape(shape), imag.reshape(shape)


def form_subgrids(masked, coords):
    count = masked.shape[0]
    cos_u, sin_u = offset_phase(coords[:, 0])
    cos_v, sin_v = offset_phase(coords[:, 1])
    vis_real = masked[:, 0, :, None]
    vis_imag = masked[:, 1, :, None]
    weight_real = vis_real * cos_u - vis_imag * sin_u
    weight_imag = vis_real * sin_u + vis_imag * cos_u
    table_real, table_imag = phase_table(NS, NS, NS, -1.0)
    table = jnp.stack(
        [
            jnp.concatenate([table_real, table_imag], axis=1),
            jnp.concatenate([-table_imag, table_real], axis=1),
        ]
    )
    row_side = jnp.einsum(
        "ikcx,cxn->ikn", jnp.stack([weight_real, weight_imag], axis=2), table, precision=HIGH
    )
    col_side = jnp.einsum(
        "ikcx,cxn->ikn", jnp.stack([cos_v, sin_v], axis=2), table, precision=HIGH
    )
    left = jnp.concatenate([row_side[:, :, :NS], row_side[:, :, NS:]], axis=1)
    right = jnp.concatenate(
        [col_side, jnp.concatenate([-col_side[:, :, NS:], col_side[:, :, :NS]], axis=2)], axis=1
    )
    full = jnp.einsum("ikp,ikn->ipn", left, right, precision=HIGH)
    return (full.reshape(count, NS, 2, NS) / (NS * NS)).astype(jnp.bfloat16)


def slot_targets(owners, tile_count, capacity):
    onehot = (owners[:, None] == jnp.arange(tile_count)[None, :]).astype(jnp.int32)
    before = jnp.cumsum(onehot, axis=0) - onehot
    slot_rank = jnp.sum(before * onehot, axis=1)
    return owners * capacity + slot_rank


def place_windows(windows, col_hi, col_lo, col_blocks):
    slots = windows.shape[0]
    wide = jnp.arange(2 * NS)
    shift = (wide[None, None, :] == col_lo[:, None, None] + jnp.arange(NS)[None, :, None])
    shifted = jnp.einsum(
        "scpq,sqw->scpw", windows, shift.astype(jnp.bfloat16), preferred_element_type=jnp.float32
    ).astype(jnp.bfloat16)
    shifted = shifted.reshape(slots, 2, NS, 2, NS)
    hit = jnp.arange(col_blocks)[:, None, None] == col_hi[None, :, None] + jnp.arange(2)[None, None, :]
    grid = jnp.einsum(
        "bsk,scpka->cpba", hit.astype(jnp.bfloat16), shifted, preferred_element_type=jnp.float32
    )
    return grid.reshape(2, NS, col_blocks * NS)


def factor_lengths(length):
    outer_len = 2 ** ((length.bit_length() - 1) // 2)
    return (outer_len, length // outer_len)


def transform_rows(grid):
    rows = grid.shape[1]
    outer_len, inner_len = factor_lengths(G)
    split = grid.reshape(2, rows, inner_len, outer_len)
    first = block_matrix(*phase_table(inner_len, inner_len, inner_len, 1.0))
    section = jnp.einsum("opba,Pobc->Pcpa", split, first, precision=HIGH)
    twiddle_real, twiddle_imag = phase_table(inner_len, outer_len, G, 1.0)
    twiddle_real = twiddle_real[:, None, :]
    twiddle_imag = twiddle_imag[:, None, :]
    turned_real = section[0] * twiddle_real - section[1] * twiddle_imag
    turned_imag = section[0] * twiddle_imag + section[1] * twiddle_real
    turned = jnp.stack([turned_real, turned_imag])
    second = block_matrix(*phase_table(outer_len, outer_len, outer_len, 1.0))
    return jnp.einsum("Ocpa,POad->dcPp", turned, second, precision=HIGH)


def transform_cols(turned):
    outer_len, inner_len = factor_lengths(G)
    first = block_matrix(*phase_table(inner_len, inner_len, inner_len, 1.0))
    section = jnp.einsum("bmoa,Pobc->Pcma", turned, first, precision=HIGH)
    twiddle_real, twiddle_imag = phase_table(inner_len, outer_len, G, 1.0)
    twiddle_real = twiddle_real[:, None, :]
    twiddle_imag = twiddle_imag[:, None, :]
    turned_real = section[0] * twiddle_real - section[1] * twiddle_imag
    turned_imag = section[0] * twiddle_imag + section[1] * twiddle_real
    second_real, second_imag = phase_table(outer_len, outer_len, outer_len, 1.0)
    second = jnp.stack([second_real, -second_imag])
    stacked = jnp.stack([turned_real, turned_imag])
    final = jnp.einsum("ocma,oad->mdc", stacked, second, precision=HIGH)
    return final.reshape(final.shape[0], G)


def per_device(samples, uv_coords, block_owner, placement_map, block_count):
    chan_count = lax.axis_size("chan")
    tile_count = lax.axis_size("tile")
    blocks = samples.shape[1]
    channels = samples.shape[2]
    steps_time = samples.shape[-1]
    group_blocks = blocks * chan_count
    capacity = max(2, 2 * group_blocks // tile_count)
    band_rows = G // tile_count
    live_mask = (jnp.arange(blocks) < block_count.reshape(())).astype(jnp.float32)
    masked = samples[0] * live_mask[:, None, None, None]
    owners = block_owner[0, :, 0]
    cols = placement_map[0, :, 1]
    meta = jnp.stack([owners, cols // NS, cols % NS], axis=1).astype(jnp.float32)
    meta = jnp.pad(meta, ((0, 0), (0, steps_time - 3)))
    meta = jnp.broadcast_to(meta[:, None, None, :], (blocks, channels, 1, steps_time))
    payload = jnp.concatenate([masked, uv_coords[0], meta], axis=2)
    arrived = lax.all_to_all(payload, "chan", split_axis=1, concat_axis=0, tiled=True)
    arrived = arrived.reshape(group_blocks, 5, steps_time)
    formed = form_subgrids(arrived[:, 0:2], arrived[:, 2:4])
    cell_count = 2 * NS * NS
    group_meta = arrived[:, 4, 0:META].astype(jnp.bfloat16)
    arrived = jnp.concatenate([formed.reshape(group_blocks, cell_count), group_meta], axis=1)
    group_owners = group_meta[:, 0].astype(jnp.int32)
    target = slot_targets(group_owners, tile_count, capacity)
    slot_count = tile_count * capacity
    pick = (jnp.arange(slot_count)[:, None] == target[None, :]).astype(jnp.bfloat16)
    outgoing = jnp.dot(pick, arrived, preferred_element_type=jnp.float32).astype(jnp.bfloat16)
    incoming = lax.all_to_all(outgoing, "tile", split_axis=0, concat_axis=0, tiled=True)
    windows = incoming[:, :cell_count].reshape(slot_count, NS, 2, NS).transpose(0, 2, 1, 3)
    col_hi = incoming[:, cell_count + 1].astype(jnp.int32)
    col_lo = incoming[:, cell_count + 2].astype(jnp.int32)
    tile_grid = place_windows(windows, col_hi, col_lo, G // NS)
    half = transform_rows(tile_grid)
    half = half.reshape(tile_count, G // tile_count, 2, band_rows).astype(jnp.bfloat16)
    turned = lax.all_to_all(half, "tile", split_axis=0, concat_axis=0, tiled=True)
    dirty_image = transform_cols(turned.astype(jnp.float32)) / G
    return dirty_image[None]


def solution(mesh):
    in_specs = (
        P("tile", "chan", None, None, None),
        P("tile", "chan", None, None, None),
        P("tile", "chan", None),
        P("tile", "chan", None),
        P("tile", "chan"),
    )
    out_specs = P("chan", "tile", None)
    return jax.shard_map(
        per_device, mesh=mesh, in_specs=in_specs, out_specs=out_specs, check_vma=False
    )
```

```python
import math

import jax
import jax.numpy as jnp
from jax import lax
from jax.sharding import PartitionSpec as P

G = 2048
NS = 32
META = 128
HIGH = lax.Precision.HIGH
HIGHEST = lax.Precision.HIGHEST


def phase_table(row_count, col_count, length, sign):
    index = jnp.arange(row_count)[:, None] * jnp.arange(col_count)[None, :] % length
    angle = sign * 2.0 * math.pi / length * index.astype(jnp.float32)
    return (jnp.cos(angle), jnp.sin(angle))


def block_matrix(real, imag):
    return jnp.stack([jnp.stack([real, -imag]), jnp.stack([imag, real])])


def complex_product(left, right):
    return (left[0] * right[0] - left[1] * right[1], left[0] * right[1] + left[1] * right[0])


def bit_select(bits, value):
    return (jnp.where(bits, value[0], 1.0), jnp.where(bits, value[1], 0.0))


def offset_phase(coord):
    theta = coord * (2.0 * math.pi / NS)
    squares = [(jnp.cos(theta)[..., None], jnp.sin(theta)[..., None])]
    for _ in range(4):
        squares.append(complex_product(squares[-1], squares[-1]))
    fine_index = jnp.arange(8)
    fine = bit_select((fine_index & 1) > 0, squares[0])
    fine = complex_product(fine, bit_select((fine_index & 2) > 0, squares[1]))
    fine = complex_product(fine, bit_select((fine_index & 4) > 0, squares[2]))
    coarse_index = jnp.arange(4)
    start = (squares[4][0], -squares[4][1])
    coarse = complex_product(start, bit_select((coarse_index & 1) > 0, squares[3]))
    coarse = complex_product(coarse, bit_select((coarse_index & 2) > 0, squares[4]))
    real = coarse[0][..., :, None] * fine[0][..., None, :] - coarse[1][..., :, None] * fine[1][..., None, :]
    imag = coarse[1][..., :, None] * fine[0][..., None, :] + coarse[0][..., :, None] * fine[1][..., None, :]
    shape = coord.shape + (NS,)
    return real.reshape(shape), imag.reshape(shape)


def form_subgrids(masked, coords):
    count = masked.shape[0]
    cos_u, sin_u = offset_phase(coords[:, 0])
    cos_v, sin_v = offset_phase(coords[:, 1])
    vis_real = masked[:, 0, :, None]
    vis_imag = masked[:, 1, :, None]
    weight_real = vis_real * cos_u - vis_imag * sin_u
    weight_imag = vis_real * sin_u + vis_imag * cos_u
    table_real, table_imag = phase_table(NS, NS, NS, -1.0)
    table = jnp.stack(
        [
            jnp.concatenate([table_real, table_imag], axis=1),
            jnp.concatenate([-table_imag, table_real], axis=1),
        ]
    )
    steps_time = masked.shape[-1]
    both = jnp.concatenate(
        [jnp.stack([weight_real, weight_imag], axis=2), jnp.stack([cos_v, sin_v], axis=2)], axis=1
    )
    both = jnp.einsum("ikcx,cxn->ikn", both, table, precision=HIGH)
    row_side, col_side = both[:, :steps_time], both[:, steps_time:]
    left = jnp.concatenate([row_side[:, :, :NS], row_side[:, :, NS:]], axis=1)
    right = jnp.concatenate(
        [col_side, jnp.concatenate([-col_side[:, :, NS:], col_side[:, :, :NS]], axis=2)], axis=1
    )
    full = jnp.einsum("ikp,ikn->ipn", left, right, precision=HIGH)
    return (full.reshape(count, NS, 2, NS) / (NS * NS)).astype(jnp.bfloat16)


def slot_targets(owners, tile_count, capacity):
    onehot = (owners[:, None] == jnp.arange(tile_count)[None, :]).astype(jnp.int32)
    before = jnp.cumsum(onehot, axis=0) - onehot
    slot_rank = jnp.sum(before * onehot, axis=1)
    return owners * capacity + slot_rank


def place_windows(windows, col_hi, col_lo, col_blocks):
    slots = windows.shape[0]
    wide = jnp.arange(2 * NS)
    shift = (wide[None, None, :] == col_lo[:, None, None] + jnp.arange(NS)[None, :, None])
    shifted = jnp.einsum(
        "scpq,sqw->scpw", windows, shift.astype(jnp.bfloat16), preferred_element_type=jnp.float32
    ).astype(jnp.bfloat16)
    shifted = shifted.reshape(slots, 2, NS, 2, NS)
    hit = jnp.arange(col_blocks)[:, None, None] == col_hi[None, :, None] + jnp.arange(2)[None, None, :]
    grid = jnp.einsum(
        "bsk,scpka->cpba", hit.astype(jnp.bfloat16), shifted, preferred_element_type=jnp.float32
    )
    return grid.reshape(2, NS, col_blocks * NS)


def factor_lengths(length):
    outer_len = 2 ** ((length.bit_length() - 1) // 2)
    return (outer_len, length // outer_len)


def transform_rows(grid):
    rows = grid.shape[1]
    outer_len, inner_len = factor_lengths(G)
    split = grid.reshape(2, rows, inner_len, outer_len)
    first = block_matrix(*phase_table(inner_len, inner_len, inner_len, 1.0))
    section = jnp.einsum("opba,Pobc->Pcpa", split, first, precision=HIGH)
    twiddle_real, twiddle_imag = phase_table(inner_len, outer_len, G, 1.0)
    twiddle_real = twiddle_real[:, None, :]
    twiddle_imag = twiddle_imag[:, None, :]
    turned_real = section[0] * twiddle_real - section[1] * twiddle_imag
    turned_imag = section[0] * twiddle_imag + section[1] * twiddle_real
    turned = jnp.stack([turned_real, turned_imag])
    second = block_matrix(*phase_table(outer_len, outer_len, outer_len, 1.0))
    return jnp.einsum("Ocpa,POad->dcPp", turned, second, precision=HIGH)


def transform_cols(turned):
    outer_len, inner_len = factor_lengths(G)
    first = block_matrix(*phase_table(inner_len, inner_len, inner_len, 1.0))
    section = jnp.einsum("bmoa,Pobc->Pcma", turned, first, precision=HIGH)
    twiddle_real, twiddle_imag = phase_table(inner_len, outer_len, G, 1.0)
    twiddle_real = twiddle_real[:, None, :]
    twiddle_imag = twiddle_imag[:, None, :]
    turned_real = section[0] * twiddle_real - section[1] * twiddle_imag
    turned_imag = section[0] * twiddle_imag + section[1] * twiddle_real
    second_real, second_imag = phase_table(outer_len, outer_len, outer_len, 1.0)
    second = jnp.stack([second_real, -second_imag])
    stacked = jnp.stack([turned_real, turned_imag])
    final = jnp.einsum("ocma,oad->mdc", stacked, second, precision=HIGH)
    return final.reshape(final.shape[0], G)


def per_device(samples, uv_coords, block_owner, placement_map, block_count):
    chan_count = lax.axis_size("chan")
    tile_count = lax.axis_size("tile")
    blocks = samples.shape[1]
    channels = samples.shape[2]
    steps_time = samples.shape[-1]
    group_blocks = blocks * chan_count
    capacity = max(2, 2 * group_blocks // tile_count)
    band_rows = G // tile_count
    live_mask = (jnp.arange(blocks) < block_count.reshape(())).astype(jnp.float32)
    masked = samples[0] * live_mask[:, None, None, None]
    owners = block_owner[0, :, 0]
    cols = placement_map[0, :, 1]
    meta = jnp.stack([owners, cols // NS, cols % NS], axis=1).astype(jnp.float32)
    meta = jnp.pad(meta, ((0, 0), (0, steps_time - 3)))
    meta = jnp.broadcast_to(meta[:, None, None, :], (blocks, channels, 1, steps_time))
    payload = jnp.concatenate([masked, uv_coords[0], meta], axis=2)
    arrived = lax.all_to_all(payload, "chan", split_axis=1, concat_axis=0, tiled=True)
    arrived = arrived.reshape(group_blocks, 5, steps_time)
    formed = form_subgrids(arrived[:, 0:2], arrived[:, 2:4])
    cell_count = 2 * NS * NS
    group_meta = arrived[:, 4, 0:META].astype(jnp.bfloat16)
    arrived = jnp.concatenate([formed.reshape(group_blocks, cell_count), group_meta], axis=1)
    group_owners = group_meta[:, 0].astype(jnp.int32)
    target = slot_targets(group_owners, tile_count, capacity)
    slot_count = tile_count * capacity
    pick = (jnp.arange(slot_count)[:, None] == target[None, :]).astype(jnp.bfloat16)
    outgoing = jnp.dot(pick, arrived, preferred_element_type=jnp.float32).astype(jnp.bfloat16)
    incoming = lax.all_to_all(outgoing, "tile", split_axis=0, concat_axis=0, tiled=True)
    windows = incoming[:, :cell_count].reshape(slot_count, NS, 2, NS).transpose(0, 2, 1, 3)
    col_hi = incoming[:, cell_count + 1].astype(jnp.int32)
    col_lo = incoming[:, cell_count + 2].astype(jnp.int32)
    tile_grid = place_windows(windows, col_hi, col_lo, G // NS)
    half = transform_rows(tile_grid)
    half = half.astype(jnp.bfloat16).reshape(tile_count, 2, G * band_rows // tile_count)
    turned = lax.all_to_all(half, "tile", split_axis=0, concat_axis=0, tiled=True)
    turned = turned.reshape(tile_count, G // tile_count, 2, band_rows)
    dirty_image = transform_cols(turned.astype(jnp.float32)) / G
    return dirty_image[None]


def solution(mesh):
    in_specs = (
        P("tile", "chan", None, None, None),
        P("tile", "chan", None, None, None),
        P("tile", "chan", None),
        P("tile", "chan", None),
        P("tile", "chan"),
    )
    out_specs = P("chan", "tile", None)
    return jax.shard_map(
        per_device, mesh=mesh, in_specs=in_specs, out_specs=out_specs, check_vma=False
    )
```

```python
import math

import jax
import jax.numpy as jnp
from jax import lax
from jax.sharding import PartitionSpec as P

G = 2048
NS = 32
META = 128
HIGH = lax.Precision.HIGH
HIGHEST = lax.Precision.HIGHEST


def phase_table(row_count, col_count, length, sign):
    index = jnp.arange(row_count)[:, None] * jnp.arange(col_count)[None, :] % length
    angle = sign * 2.0 * math.pi / length * index.astype(jnp.float32)
    return (jnp.cos(angle), jnp.sin(angle))


def block_matrix(real, imag):
    return jnp.stack([jnp.stack([real, -imag]), jnp.stack([imag, real])])


def complex_product(left, right):
    return (left[0] * right[0] - left[1] * right[1], left[0] * right[1] + left[1] * right[0])


def bit_select(bits, value):
    return (jnp.where(bits, value[0], 1.0), jnp.where(bits, value[1], 0.0))


def offset_phase(coord):
    theta = coord * (2.0 * math.pi / NS)
    squares = [(jnp.cos(theta)[..., None], jnp.sin(theta)[..., None])]
    for _ in range(4):
        squares.append(complex_product(squares[-1], squares[-1]))
    fine_index = jnp.arange(8)
    fine = bit_select((fine_index & 1) > 0, squares[0])
    fine = complex_product(fine, bit_select((fine_index & 2) > 0, squares[1]))
    fine = complex_product(fine, bit_select((fine_index & 4) > 0, squares[2]))
    coarse_index = jnp.arange(4)
    start = (squares[4][0], -squares[4][1])
    coarse = complex_product(start, bit_select((coarse_index & 1) > 0, squares[3]))
    coarse = complex_product(coarse, bit_select((coarse_index & 2) > 0, squares[4]))
    real = coarse[0][..., :, None] * fine[0][..., None, :] - coarse[1][..., :, None] * fine[1][..., None, :]
    imag = coarse[1][..., :, None] * fine[0][..., None, :] + coarse[0][..., :, None] * fine[1][..., None, :]
    shape = coord.shape + (NS,)
    return real.reshape(shape), imag.reshape(shape)


def form_subgrids(masked, coords):
    count = masked.shape[0]
    cos_u, sin_u = offset_phase(coords[:, 0])
    cos_v, sin_v = offset_phase(coords[:, 1])
    vis_real = masked[:, 0, :, None]
    vis_imag = masked[:, 1, :, None]
    weight_real = vis_real * cos_u - vis_imag * sin_u
    weight_imag = vis_real * sin_u + vis_imag * cos_u
    table_real, table_imag = phase_table(NS, NS, NS, -1.0)
    table = jnp.stack(
        [
            jnp.concatenate([table_real, table_imag], axis=1),
            jnp.concatenate([-table_imag, table_real], axis=1),
        ]
    )
    steps_time = masked.shape[-1]
    both = jnp.concatenate(
        [jnp.stack([weight_real, weight_imag], axis=2), jnp.stack([cos_v, sin_v], axis=2)], axis=1
    )
    both = jnp.einsum("ikcx,cxn->ikn", both, table, precision=HIGH)
    row_side, col_side = both[:, :steps_time], both[:, steps_time:]
    left = jnp.concatenate([row_side[:, :, :NS], row_side[:, :, NS:]], axis=1)
    right = jnp.concatenate(
        [col_side, jnp.concatenate([-col_side[:, :, NS:], col_side[:, :, :NS]], axis=2)], axis=1
    )
    full = jnp.einsum("ikp,ikn->ipn", left, right, precision=HIGH)
    return (full.reshape(count, NS, 2, NS) / (NS * NS)).astype(jnp.bfloat16)


def slot_targets(owners, tile_count, capacity):
    onehot = (owners[:, None] == jnp.arange(tile_count)[None, :]).astype(jnp.int32)
    before = jnp.cumsum(onehot, axis=0) - onehot
    slot_rank = jnp.sum(before * onehot, axis=1)
    return owners * capacity + slot_rank


def place_windows(windows, col_hi, col_lo, col_blocks):
    slots = windows.shape[0]
    wide = jnp.arange(2 * NS)
    shift = (wide[None, None, :] == col_lo[:, None, None] + jnp.arange(NS)[None, :, None])
    shifted = jnp.einsum(
        "scpq,sqw->scpw", windows, shift.astype(jnp.bfloat16), preferred_element_type=jnp.float32
    ).astype(jnp.bfloat16)
    shifted = shifted.reshape(slots, 2, NS, 2, NS)
    hit = jnp.arange(col_blocks)[:, None, None] == col_hi[None, :, None] + jnp.arange(2)[None, None, :]
    grid = jnp.einsum(
        "bsk,scpka->cpba", hit.astype(jnp.bfloat16), shifted, preferred_element_type=jnp.float32
    )
    return grid.reshape(2, NS, col_blocks * NS)


def factor_lengths(length):
    outer_len = 2 ** ((length.bit_length() - 1) // 2)
    return (outer_len, length // outer_len)


def transform_rows(grid):
    rows = grid.shape[1]
    outer_len, inner_len = factor_lengths(G)
    split = grid.reshape(2, rows, inner_len, outer_len)
    first = block_matrix(*phase_table(inner_len, inner_len, inner_len, 1.0))
    section = jnp.einsum("opba,Pobc->Pcpa", split, first, precision=HIGH)
    twiddle_real, twiddle_imag = phase_table(inner_len, outer_len, G, 1.0)
    twiddle_real = twiddle_real[:, None, :]
    twiddle_imag = twiddle_imag[:, None, :]
    turned_real = section[0] * twiddle_real - section[1] * twiddle_imag
    turned_imag = section[0] * twiddle_imag + section[1] * twiddle_real
    turned = jnp.stack([turned_real, turned_imag])
    second = block_matrix(*phase_table(outer_len, outer_len, outer_len, 1.0))
    return jnp.einsum("Ocpa,POad->dcPp", turned, second, precision=HIGH)


def transform_cols(turned):
    outer_len, inner_len = factor_lengths(G)
    first = block_matrix(*phase_table(inner_len, inner_len, inner_len, 1.0))
    section = jnp.einsum("bmoa,Pobc->Pcma", turned, first, precision=HIGH)
    twiddle_real, twiddle_imag = phase_table(inner_len, outer_len, G, 1.0)
    twiddle_real = twiddle_real[:, None, :]
    twiddle_imag = twiddle_imag[:, None, :]
    turned_real = section[0] * twiddle_real - section[1] * twiddle_imag
    turned_imag = section[0] * twiddle_imag + section[1] * twiddle_real
    second_real, second_imag = phase_table(outer_len, outer_len, outer_len, 1.0)
    second = jnp.stack([second_real, -second_imag])
    stacked = jnp.stack([turned_real, turned_imag])
    final = jnp.einsum("ocma,oad->mdc", stacked, second, precision=HIGH)
    return final.reshape(final.shape[0], G)


def per_device(samples, uv_coords, block_owner, placement_map, block_count):
    chan_count = lax.axis_size("chan")
    tile_count = lax.axis_size("tile")
    blocks = samples.shape[1]
    channels = samples.shape[2]
    steps_time = samples.shape[-1]
    group_blocks = blocks * chan_count
    capacity = max(2, 2 * group_blocks // tile_count)
    band_rows = G // tile_count
    live_mask = (jnp.arange(blocks) < block_count.reshape(())).astype(jnp.float32)
    masked = samples[0] * live_mask[:, None, None, None]
    owners = block_owner[0, :, 0]
    cols = placement_map[0, :, 1]
    meta = jnp.stack([owners, cols], axis=1).astype(jnp.float32)
    meta = jnp.pad(meta, ((0, 0), (0, steps_time - 2)))
    meta = jnp.broadcast_to(meta[:, None, None, :], (blocks, channels, 1, steps_time))
    payload = jnp.concatenate([masked, uv_coords[0], meta], axis=2)
    arrived = lax.all_to_all(payload, "chan", split_axis=1, concat_axis=0, tiled=True)
    arrived = arrived.reshape(group_blocks, 5, steps_time)
    formed = form_subgrids(arrived[:, 0:2], arrived[:, 2:4])
    cell_count = 2 * NS * NS
    group_cols = arrived[:, 4, 1]
    col_hi = jnp.floor(group_cols / NS)
    col_lo = group_cols - NS * col_hi
    group_meta = jnp.stack([arrived[:, 4, 0], col_hi, col_lo], axis=1)
    group_meta = jnp.pad(group_meta, ((0, 0), (0, META - 3))).astype(jnp.bfloat16)
    arrived = jnp.concatenate([formed.reshape(group_blocks, cell_count), group_meta], axis=1)
    group_owners = group_meta[:, 0].astype(jnp.int32)
    target = slot_targets(group_owners, tile_count, capacity)
    slot_count = tile_count * capacity
    pick = (jnp.arange(slot_count)[:, None] == target[None, :]).astype(jnp.bfloat16)
    outgoing = jnp.dot(pick, arrived, preferred_element_type=jnp.float32).astype(jnp.bfloat16)
    incoming = lax.all_to_all(outgoing, "tile", split_axis=0, concat_axis=0, tiled=True)
    windows = incoming[:, :cell_count].reshape(slot_count, NS, 2, NS).transpose(0, 2, 1, 3)
    col_hi = incoming[:, cell_count + 1].astype(jnp.int32)
    col_lo = incoming[:, cell_count + 2].astype(jnp.int32)
    tile_grid = place_windows(windows, col_hi, col_lo, G // NS)
    half = transform_rows(tile_grid)
    half = half.astype(jnp.bfloat16).reshape(tile_count, 2, G * band_rows // tile_count)
    turned = lax.all_to_all(half, "tile", split_axis=0, concat_axis=0, tiled=True)
    turned = turned.reshape(tile_count, G // tile_count, 2, band_rows)
    dirty_image = transform_cols(turned.astype(jnp.float32)) / G
    return dirty_image[None]


def solution(mesh):
    in_specs = (
        P("tile", "chan", None, None, None),
        P("tile", "chan", None, None, None),
        P("tile", "chan", None),
        P("tile", "chan", None),
        P("tile", "chan"),
    )
    out_specs = P("chan", "tile", None)
    return jax.shard_map(
        per_device, mesh=mesh, in_specs=in_specs, out_specs=out_specs, check_vma=False
    )
```

```python
import math

import jax
import jax.numpy as jnp
from jax import lax
from jax.sharding import PartitionSpec as P

G = 2048
NS = 32
META = 128
HIGH = lax.Precision.HIGH
HIGHEST = lax.Precision.HIGHEST


def phase_table(row_count, col_count, length, sign):
    index = jnp.arange(row_count)[:, None] * jnp.arange(col_count)[None, :] % length
    angle = sign * 2.0 * math.pi / length * index.astype(jnp.float32)
    return (jnp.cos(angle), jnp.sin(angle))


def block_matrix(real, imag):
    return jnp.stack([jnp.stack([real, -imag]), jnp.stack([imag, real])])


def complex_product(left, right):
    return (left[0] * right[0] - left[1] * right[1], left[0] * right[1] + left[1] * right[0])


def bit_select(bits, value):
    return (jnp.where(bits, value[0], 1.0), jnp.where(bits, value[1], 0.0))


def offset_phase(coord):
    theta = coord * (2.0 * math.pi / NS)
    squares = [(jnp.cos(theta)[..., None], jnp.sin(theta)[..., None])]
    for _ in range(4):
        squares.append(complex_product(squares[-1], squares[-1]))
    fine_index = jnp.arange(8)
    fine = bit_select((fine_index & 1) > 0, squares[0])
    fine = complex_product(fine, bit_select((fine_index & 2) > 0, squares[1]))
    fine = complex_product(fine, bit_select((fine_index & 4) > 0, squares[2]))
    coarse_index = jnp.arange(4)
    start = (squares[4][0], -squares[4][1])
    coarse = complex_product(start, bit_select((coarse_index & 1) > 0, squares[3]))
    coarse = complex_product(coarse, bit_select((coarse_index & 2) > 0, squares[4]))
    real = coarse[0][..., :, None] * fine[0][..., None, :] - coarse[1][..., :, None] * fine[1][..., None, :]
    imag = coarse[1][..., :, None] * fine[0][..., None, :] + coarse[0][..., :, None] * fine[1][..., None, :]
    shape = coord.shape + (NS,)
    return real.reshape(shape), imag.reshape(shape)


def form_subgrids(masked, coords):
    count = masked.shape[0]
    cos_u, sin_u = offset_phase(coords[:, 0])
    cos_v, sin_v = offset_phase(coords[:, 1])
    vis_real = masked[:, 0, :, None]
    vis_imag = masked[:, 1, :, None]
    weight_real = vis_real * cos_u - vis_imag * sin_u
    weight_imag = vis_real * sin_u + vis_imag * cos_u
    table_real, table_imag = phase_table(NS, NS, NS, -1.0)
    table = jnp.stack(
        [
            jnp.concatenate([table_real, table_imag], axis=1),
            jnp.concatenate([-table_imag, table_real], axis=1),
        ]
    )
    steps_time = masked.shape[-1]
    both = jnp.concatenate(
        [jnp.stack([weight_real, weight_imag], axis=2), jnp.stack([cos_v, sin_v], axis=2)], axis=1
    )
    both = jnp.einsum("ikcx,cxn->ikn", both, table, precision=HIGH)
    row_side, col_side = both[:, :steps_time], both[:, steps_time:]
    left = jnp.concatenate([row_side[:, :, :NS], row_side[:, :, NS:]], axis=1)
    right = jnp.concatenate(
        [col_side, jnp.concatenate([-col_side[:, :, NS:], col_side[:, :, :NS]], axis=2)], axis=1
    )
    full = jnp.einsum("ikp,ikn->ipn", left, right, precision=HIGH)
    return (full.reshape(count, NS, 2, NS) / (NS * NS)).astype(jnp.bfloat16)


def slot_targets(owners, tile_count, capacity):
    count = owners.shape[0]
    onehot = (owners[:, None] == jnp.arange(tile_count)[None, :]).astype(jnp.bfloat16)
    earlier = (jnp.arange(count)[None, :] < jnp.arange(count)[:, None]).astype(jnp.bfloat16)
    before = jnp.dot(earlier, onehot, preferred_element_type=jnp.float32)
    slot_rank = jnp.sum(before * onehot.astype(jnp.float32), axis=1).astype(jnp.int32)
    return owners * capacity + slot_rank


def place_windows(windows, col_hi, col_lo, col_blocks):
    slots = windows.shape[0]
    wide = jnp.arange(2 * NS)
    shift = (wide[None, None, :] == col_lo[:, None, None] + jnp.arange(NS)[None, :, None])
    shifted = jnp.einsum(
        "scpq,sqw->scpw", windows, shift.astype(jnp.bfloat16), preferred_element_type=jnp.float32
    ).astype(jnp.bfloat16)
    shifted = shifted.reshape(slots, 2, NS, 2, NS)
    hit = jnp.arange(col_blocks)[:, None, None] == col_hi[None, :, None] + jnp.arange(2)[None, None, :]
    grid = jnp.einsum(
        "bsk,scpka->cpba", hit.astype(jnp.bfloat16), shifted, preferred_element_type=jnp.float32
    )
    return grid.reshape(2, NS, col_blocks * NS)


def factor_lengths(length):
    outer_len = 2 ** ((length.bit_length() - 1) // 2)
    return (outer_len, length // outer_len)


def transform_rows(grid):
    rows = grid.shape[1]
    outer_len, inner_len = factor_lengths(G)
    split = grid.reshape(2, rows, inner_len, outer_len)
    first = block_matrix(*phase_table(inner_len, inner_len, inner_len, 1.0))
    section = jnp.einsum("opba,Pobc->Pcpa", split, first, precision=HIGH)
    twiddle_real, twiddle_imag = phase_table(inner_len, outer_len, G, 1.0)
    twiddle_real = twiddle_real[:, None, :]
    twiddle_imag = twiddle_imag[:, None, :]
    turned_real = section[0] * twiddle_real - section[1] * twiddle_imag
    turned_imag = section[0] * twiddle_imag + section[1] * twiddle_real
    turned = jnp.stack([turned_real, turned_imag])
    second = block_matrix(*phase_table(outer_len, outer_len, outer_len, 1.0))
    return jnp.einsum("Ocpa,POad->dcPp", turned, second, precision=HIGH)


def transform_cols(turned):
    outer_len, inner_len = factor_lengths(G)
    first = block_matrix(*phase_table(inner_len, inner_len, inner_len, 1.0))
    section = jnp.einsum("bmoa,Pobc->Pcma", turned, first, precision=HIGH)
    twiddle_real, twiddle_imag = phase_table(inner_len, outer_len, G, 1.0)
    twiddle_real = twiddle_real[:, None, :]
    twiddle_imag = twiddle_imag[:, None, :]
    turned_real = section[0] * twiddle_real - section[1] * twiddle_imag
    turned_imag = section[0] * twiddle_imag + section[1] * twiddle_real
    second_real, second_imag = phase_table(outer_len, outer_len, outer_len, 1.0)
    second = jnp.stack([second_real, -second_imag])
    stacked = jnp.stack([turned_real, turned_imag])
    final = jnp.einsum("ocma,oad->mdc", stacked, second, precision=HIGH)
    return final.reshape(final.shape[0], G)


def per_device(samples, uv_coords, block_owner, placement_map, block_count):
    chan_count = lax.axis_size("chan")
    tile_count = lax.axis_size("tile")
    blocks = samples.shape[1]
    channels = samples.shape[2]
    steps_time = samples.shape[-1]
    group_blocks = blocks * chan_count
    capacity = max(2, 2 * group_blocks // tile_count)
    band_rows = G // tile_count
    live_mask = (jnp.arange(blocks) < block_count.reshape(())).astype(jnp.float32)
    masked = samples[0] * live_mask[:, None, None, None]
    owners = block_owner[0, :, 0]
    cols = placement_map[0, :, 1]
    meta = jnp.stack([owners, cols], axis=1).astype(jnp.float32)
    meta = jnp.pad(meta, ((0, 0), (0, steps_time - 2)))
    meta = jnp.broadcast_to(meta[:, None, None, :], (blocks, channels, 1, steps_time))
    payload = jnp.concatenate([masked, uv_coords[0], meta], axis=2)
    arrived = lax.all_to_all(payload, "chan", split_axis=1, concat_axis=0, tiled=True)
    arrived = arrived.reshape(group_blocks, 5, steps_time)
    formed = form_subgrids(arrived[:, 0:2], arrived[:, 2:4])
    cell_count = 2 * NS * NS
    group_cols = arrived[:, 4, 1]
    col_hi = jnp.floor(group_cols / NS)
    col_lo = group_cols - NS * col_hi
    group_meta = jnp.stack([arrived[:, 4, 0], col_hi, col_lo], axis=1)
    group_meta = jnp.pad(group_meta, ((0, 0), (0, META - 3))).astype(jnp.bfloat16)
    arrived = jnp.concatenate([formed.reshape(group_blocks, cell_count), group_meta], axis=1)
    group_owners = group_meta[:, 0].astype(jnp.int32)
    target = slot_targets(group_owners, tile_count, capacity)
    slot_count = tile_count * capacity
    pick = (jnp.arange(slot_count)[:, None] == target[None, :]).astype(jnp.bfloat16)
    outgoing = jnp.dot(pick, arrived, preferred_element_type=jnp.float32).astype(jnp.bfloat16)
    incoming = lax.all_to_all(outgoing, "tile", split_axis=0, concat_axis=0, tiled=True)
    windows = incoming[:, :cell_count].reshape(slot_count, NS, 2, NS).transpose(0, 2, 1, 3)
    col_hi = incoming[:, cell_count + 1].astype(jnp.int32)
    col_lo = incoming[:, cell_count + 2].astype(jnp.int32)
    tile_grid = place_windows(windows, col_hi, col_lo, G // NS)
    half = transform_rows(tile_grid)
    half = half.astype(jnp.bfloat16).reshape(tile_count, 2, G * band_rows // tile_count)
    turned = lax.all_to_all(half, "tile", split_axis=0, concat_axis=0, tiled=True)
    turned = turned.reshape(tile_count, G // tile_count, 2, band_rows)
    dirty_image = transform_cols(turned.astype(jnp.float32)) / G
    return dirty_image[None]


def solution(mesh):
    in_specs = (
        P("tile", "chan", None, None, None),
        P("tile", "chan", None, None, None),
        P("tile", "chan", None),
        P("tile", "chan", None),
        P("tile", "chan"),
    )
    out_specs = P("chan", "tile", None)
    return jax.shard_map(
        per_device, mesh=mesh, in_specs=in_specs, out_specs=out_specs, check_vma=False
    )
```
